32 devices in a mesh: pp: 2 (over y), ep: 16 (over z, x, core).
Axes of the slice: x: 2, y: 2, z: 4, core: 2. Of those that a mesh axis runs over, the one named last changes fastest.
Arguments:
- fwd_input: bfloat16 [2, 512, 7168], P('pp', 'ep'), may hold values from -6 to 6
- fwd_experts: int32 [2, 512, 2], P('pp', 'ep'), may hold values from 0 to 3, all different within a row; in each aligned block of 32 rows (0 to 31, 32 to 63, ..., all dimensions but the last counted through in order) at most 24 rows name the same one
- fwd_gates: float32 [2, 512, 2], P('pp', 'ep'), may hold values from 0.1 to 1
- bwd_input: bfloat16 [2, 512, 7168], P('pp', 'ep'), may hold values from -6 to 6
- bwd_grad: bfloat16 [2, 512, 7168], P('pp', 'ep'), may hold values from -6 to 6
- bwd_experts: int32 [2, 512, 2], P('pp', 'ep'), may hold values from 0 to 3, all different within a row; in each aligned block of 32 rows (0 to 31, 32 to 63, ..., all dimensions but the last counted through in order) at most 24 rows name the same one
- bwd_gates: float32 [2, 512, 2], P('pp', 'ep'), may hold values from 0.1 to 1
- gate_proj: bfloat16 [2, 7168, 4096], P('pp', None, 'ep'), may hold values from -0.0625 to 0.0625
- up_proj: bfloat16 [2, 7168, 4096], P('pp', None, 'ep'), may hold values from -0.0625 to 0.0625
- down_proj: bfloat16 [2, 4096, 7168], P('pp', 'ep'), may hold values from -0.1875 to 0.1875
Outputs:
- next_section_input: bfloat16 [2, 512, 7168], P('pp', 'ep')
- prev_section_grad: bfloat16 [2, 512, 7168], P('pp', 'ep')
The draws below stay inside these ranges and needn't reach their ends.
Inputs may be any that keep to these rules, and one draw needn't show every extreme that they name: `fwd_experts`: each token names 2 different experts; in each device's aligned block of 32 tokens no expert is named more than 24 times, a bound that some block reaches. `bwd_experts`: each token names 2 different experts; in each device's aligned block of 32 tokens no expert is named more than 24 times, a bound that some block reaches.
All inputs are finite; a program needn't handle non-finite values.
Results may differ from the reference program's by a relative error of at most 0.0075.
Values may be sent and summed in bfloat16 or wider, within the bound.
No kernel may reach another device: no remote copies, remote signals or barrier semaphores. Data moves between devices by JAX's collectives and lax.ppermute only.
A program may use at most 128 MiB of HBM per device.

```python
import math
import jax
import jax.numpy as jnp
import numpy as np
from jax import lax

D = 7168
FF = 1024
GROUP = 4
TOPK = 2
TOK_DEV = 32
EXPERTS = 4
CAP = 24
TOKENS = 512
SECTIONS = 2
N_EP = 16


def level_of(rng, extent, split, smallest, top_value):
    def one(dim, shards_of):
        draws = jax.random.uniform(jax.random.fold_in(jax.random.fold_in(rng, 6), dim), (shards_of,), jnp.float32, smallest / len(split), top_value / len(split))
        return jnp.repeat(jnp.exp(draws), extent[dim] // shards_of).reshape((-1,) + (1,) * (len(extent) - dim - 1))

    level = one(*split[0])
    for cut in split[1:]:
        level = level * one(*cut)
    return level


def routed_block(own_key, own, number, rows, amount, top, reach, slope):
    ranking = jax.random.permutation(own_key, amount)
    crowded, common = shares(amount, rows * top, reach, slope, True), shares(amount, rows * top, reach, slope, False)
    places = jnp.arange(amount)

    def named(tallies, turn):
        used = int((tallies > 0).sum())
        fixed = max(1, used // 4)
        passed = fixed + (places - fixed + turn * (used - fixed)) % max(1, amount - fixed)
        return jnp.zeros((amount,), jnp.int32).at[ranking[jnp.where(places < fixed, places, passed)]].set(jnp.asarray(tallies, jnp.int32))

    tallies = jnp.where(number % 4 == 0, named(crowded, number // 4), named(common, number - number // 4 - 1))
    mixed = jax.random.permutation(jax.random.fold_in(own, 3), amount)
    donor, taker = mixed[0:amount // 2 * 2:2], mixed[1:amount // 2 * 2:2]
    room = jnp.minimum(tallies[donor] - 1, reach - tallies[taker]) // 2
    room = jnp.where((donor == ranking[0]) | (taker == ranking[0]) | (tallies[taker] == 0), 0, jnp.maximum(room, 0))
    passed = jax.random.randint(jax.random.fold_in(own, 4), (amount // 2,), 0, 1 << 20) % (room + 1)
    tallies = tallies.at[donor].add(-passed).at[taker].add(passed)
    labels = jnp.searchsorted(jnp.cumsum(tallies), jnp.arange(rows * top), side="right").astype(jnp.int32)
    grid = labels.reshape(top, rows).T
    grid = grid[jax.random.permutation(jax.random.fold_in(own, 1), rows)]
    turn = jax.random.randint(jax.random.fold_in(own, 2), (rows, 1), 0, top)
    return jnp.take_along_axis(grid, (jnp.arange(top)[None, :] + turn) % top, axis=1)


def shares(count, total, bound, lean, full):
    loads = [(1 << 20) // math.isqrt(grade ** lean) + 1 for grade in range(1, count + 1)]
    largest = bound if full else min(bound, max(-(-total // count), total * loads[0] // sum(loads)))
    least = 1 if total - largest >= count - 1 else 0
    given, spare = [largest] + [least] * (count - 1), total - largest - least * (count - 1)
    while spare > 0:
        movable = [i for i in range(1, count) if given[i] < largest] or [i for i in range(1, count) if given[i] < bound]
        whole, budget = sum([loads[i] for i in movable]), spare
        for i in movable:
            more = min(bound - given[i], max(1, budget * loads[i] // whole), spare)
            given[i] = given[i] + more
            spare = spare - more
    return np.array(given)


def scatter_about(key, extent, scale, limit, cuts=(), kind=jnp.bfloat16):
    entries = scale * jax.random.normal(key, extent, jnp.float32)
    if cuts:
        entries = entries * level_of(key, extent, cuts, -0.22, 0.18)
    return jnp.clip(entries, -limit, limit).astype(kind)


def setup_inputs(seed: int = 0) -> dict:
    arg_keys = jax.random.split(jax.random.key(seed), 11)
    fwd_input = scatter_about(arg_keys[0], (SECTIONS, TOKENS, D), 1.0, 6.0, ((0, 2), (1, 16)))
    fwd_experts_keys = jax.random.split(jax.random.fold_in(arg_keys[1], 1), SECTIONS * TOKENS // TOK_DEV)
    fwd_experts_turns = jax.random.permutation(jax.random.fold_in(arg_keys[1], 3), SECTIONS * TOKENS // TOK_DEV)
    fwd_experts = jax.vmap(lambda own, number: routed_block(jax.random.fold_in(arg_keys[1], 2), own, number, TOK_DEV, EXPERTS, TOPK, CAP, 2))(fwd_experts_keys, fwd_experts_turns).reshape((SECTIONS, TOKENS, TOPK))
    fwd_gates = jnp.clip(0.1 + 0.9 * jax.random.uniform(arg_keys[2], (SECTIONS, TOKENS, TOPK), jnp.float32) ** level_of(arg_keys[2], (SECTIONS, TOKENS, TOPK), ((0, 2), (1, 16)), -0.2, 0.2), 0.1, 1.0)
    bwd_input = scatter_about(arg_keys[3], (SECTIONS, TOKENS, D), 1.0, 6.0, ((0, 2), (1, 16)))
    bwd_grad = scatter_about(arg_keys[4], (SECTIONS, TOKENS, D), 1.0, 6.0, ((0, 2), (1, 16)))
    bwd_experts_keys = jax.random.split(jax.random.fold_in(arg_keys[5], 1), SECTIONS * TOKENS // TOK_DEV)
    bwd_experts_turns = jax.random.permutation(jax.random.fold_in(arg_keys[5], 3), SECTIONS * TOKENS // TOK_DEV)
    bwd_experts = jax.vmap(lambda own, number: routed_block(jax.random.fold_in(arg_keys[5], 2), own, number, TOK_DEV, EXPERTS, TOPK, CAP, 2))(bwd_experts_keys, bwd_experts_turns).reshape((SECTIONS, TOKENS, TOPK))
    bwd_gates = jnp.clip(0.1 + 0.9 * jax.random.uniform(arg_keys[6], (SECTIONS, TOKENS, TOPK), jnp.float32) ** level_of(arg_keys[6], (SECTIONS, TOKENS, TOPK), ((0, 2), (1, 16)), -0.2, 0.2), 0.1, 1.0)
    gate_proj = scatter_about(arg_keys[7], (SECTIONS, D, EXPERTS * FF), D ** -0.5, 0.0625, ((0, 2), (2, 16)))
    up_proj = scatter_about(arg_keys[8], (SECTIONS, D, EXPERTS * FF), D ** -0.5, 0.0625, ((0, 2), (2, 16)))
    down_proj = scatter_about(arg_keys[9], (SECTIONS, EXPERTS * FF, D), FF ** -0.5, 0.1875, ((0, 2), (1, 16)))
    return dict(fwd_input=fwd_input, fwd_experts=fwd_experts, fwd_gates=fwd_gates, bwd_input=bwd_input, bwd_grad=bwd_grad, bwd_experts=bwd_experts, bwd_gates=bwd_gates, gate_proj=gate_proj, up_proj=up_proj, down_proj=down_proj)


def slot_rows(ids):
    pairs = ids.reshape(N_EP, TOK_DEV * TOPK)
    hot = (pairs[:, :, None] == jnp.arange(EXPERTS, dtype=jnp.int32)[None, None, :]).astype(jnp.int32)
    before = jnp.cumsum(hot, axis=1) - hot
    slot = jnp.sum(hot * before, axis=2).reshape(TOKENS, TOPK)
    block = (jnp.arange(TOKENS, dtype=jnp.int32) // TOK_DEV)[:, None]
    return (block * CAP + slot).astype(jnp.int32)


def place(rows_in, ids, where_rows):
    width = rows_in.shape[1]
    spread = jnp.broadcast_to(rows_in[:, None, :], (TOKENS, TOPK, width))
    empty = jnp.zeros((EXPERTS, N_EP * CAP, width), jnp.bfloat16)
    return empty.at[ids, where_rows].set(spread)


def combine(base, outs, ids, where_rows, gates):
    picked = outs[ids, where_rows].astype(jnp.float32)
    total = base.astype(jnp.float32) + jnp.sum(gates[:, :, None] * picked, axis=1)
    return total.astype(jnp.bfloat16)


def expert_forward(items):
    rows_in, w_gate, w_up, w_down = items
    hi = lax.Precision.HIGHEST
    xs = rows_in.astype(jnp.float32)
    g = jnp.einsum("rd,dgh->rgh", xs, w_gate.astype(jnp.float32), precision=hi)
    u = jnp.einsum("rd,dgh->rgh", xs, w_up.astype(jnp.float32), precision=hi)
    hidden = (g * jax.nn.sigmoid(g) * u).astype(jnp.bfloat16)
    part = jnp.einsum("rgh,ghd->rgd", hidden.astype(jnp.float32), w_down.astype(jnp.float32), precision=hi)
    part = part.astype(jnp.bfloat16).astype(jnp.float32)
    return jnp.sum(part, axis=1).astype(jnp.bfloat16)


def expert_backward(items):
    rows_in, rows_grad, w_gate, w_up, w_down = items
    hi = lax.Precision.HIGHEST
    xs = rows_in.astype(jnp.float32)
    wg = w_gate.astype(jnp.float32)
    wu = w_up.astype(jnp.float32)
    g = jnp.einsum("rd,dgh->rgh", xs, wg, precision=hi)
    u = jnp.einsum("rd,dgh->rgh", xs, wu, precision=hi)
    dh = jnp.einsum("rd,ghd->rgh", rows_grad.astype(jnp.float32), w_down.astype(jnp.float32), precision=hi)
    sig = jax.nn.sigmoid(g)
    grad_gate = (dh * u * sig * (1.0 + g * (1.0 - sig))).astype(jnp.bfloat16)
    grad_up = (dh * g * sig).astype(jnp.bfloat16)
    part = jnp.einsum("rgh,dgh->rgd", grad_gate.astype(jnp.float32), wg, precision=hi)
    part = part + jnp.einsum("rgh,dgh->rgd", grad_up.astype(jnp.float32), wu, precision=hi)
    part = part.astype(jnp.bfloat16).astype(jnp.float32)
    return jnp.sum(part, axis=1).astype(jnp.bfloat16)


def one_section(items):
    (f_in, f_ids, f_gates, b_in, b_grad, b_ids, b_gates, gate_w, up_w, down_w) = items
    hid = FF // GROUP
    wg = gate_w.reshape(D, EXPERTS, GROUP, hid).transpose(1, 0, 2, 3)
    wu = up_w.reshape(D, EXPERTS, GROUP, hid).transpose(1, 0, 2, 3)
    wd = down_w.reshape(EXPERTS, GROUP, hid, D)
    f_rows = slot_rows(f_ids)
    f_sent = place(f_in, f_ids, f_rows)
    f_outs = lax.map(expert_forward, (f_sent, wg, wu, wd))
    f_result = combine(f_in, f_outs, f_ids, f_rows, f_gates)
    b_rows = slot_rows(b_ids)
    b_sent_in = place(b_in, b_ids, b_rows)
    b_sent_grad = place(b_grad, b_ids, b_rows)
    b_outs = lax.map(expert_backward, (b_sent_in, b_sent_grad, wg, wu, wd))
    b_result = combine(b_grad, b_outs, b_ids, b_rows, b_gates)
    return f_result, b_result


def reference(fwd_input, fwd_experts, fwd_gates, bwd_input, bwd_grad, bwd_experts, bwd_gates, gate_proj, up_proj, down_proj):
    f_all, b_all = lax.map(one_section, (fwd_input, fwd_experts, fwd_gates, bwd_input, bwd_grad, bwd_experts, bwd_gates, gate_proj, up_proj, down_proj))
    return jnp.roll(f_all, 1, axis=0), jnp.roll(b_all, -1, axis=0)
```

```python
import jax
import jax.numpy as jnp
from jax import lax
from jax.sharding import Mesh
from jax.sharding import PartitionSpec as P

GROUP = 4
TOPK = 2
EP = ("z", "x", "c")


def swap(value, axis):
    return lax.ppermute(value, axis, [(0, 1), (1, 0)])


def passed_along(value, axis, steps):
    count = lax.axis_size(axis)
    pairs = [(source, (source + steps) % count) for source in range(count)]
    return lax.ppermute(value, axis, pairs)


def routing(ids, gates, experts, capacity):
    pairs = ids.reshape(-1)
    hot = (pairs[:, None] == jnp.arange(experts, dtype=jnp.int32)[None, :]).astype(jnp.int32)
    before = jnp.cumsum(hot, axis=0) - hot
    slot = jnp.sum(hot * before, axis=1)
    target = (pairs * capacity + slot).reshape(ids.shape)
    columns = jnp.arange(experts * capacity, dtype=jnp.int32)
    match = (target[:, :, None] == columns[None, None, :]).astype(jnp.float32)
    select = jnp.sum(match, axis=1).astype(jnp.bfloat16)
    weights = jnp.sum(gates[:, :, None] * match, axis=1)
    return (select, weights)


def into_slots(select, rows_in):
    placed = lax.dot_general(
        select, rows_in, (((0,), (0,)), ((), ())), preferred_element_type=jnp.float32
    )
    return placed.astype(jnp.bfloat16)


def forward_rows(rows_in, w_gate, w_up, w_down):
    g = jnp.dot(rows_in, w_gate, preferred_element_type=jnp.float32)
    u = jnp.dot(rows_in, w_up, preferred_element_type=jnp.float32)
    hidden = (g * jax.nn.sigmoid(g) * u).astype(jnp.bfloat16)
    return jnp.dot(hidden, w_down, preferred_element_type=jnp.float32).astype(jnp.bfloat16)


def backward_rows(rows_all, w_gate, w_up, w_down):
    width = w_gate.shape[0]
    rows_in = rows_all[:, :width]
    rows_grad = rows_all[:, width:]
    g = jnp.dot(rows_in, w_gate, preferred_element_type=jnp.float32)
    u = jnp.dot(rows_in, w_up, preferred_element_type=jnp.float32)
    dh = lax.dot_general(
        rows_grad, w_down, (((1,), (1,)), ((), ())), preferred_element_type=jnp.float32
    )
    sig = jax.nn.sigmoid(g)
    grad_gate = (dh * u * sig * (1.0 + g * (1.0 - sig))).astype(jnp.bfloat16)
    grad_up = (dh * g * sig).astype(jnp.bfloat16)
    part = lax.dot_general(
        grad_gate, w_gate, (((1,), (1,)), ((), ())), preferred_element_type=jnp.float32
    )
    part = part + lax.dot_general(
        grad_up, w_up, (((1,), (1,)), ((), ())), preferred_element_type=jnp.float32
    )
    return part.astype(jnp.bfloat16)


def dispatch(slots):
    received = lax.all_to_all(slots, "z", 0, 0, tiled=True)
    across = jnp.stack([received, swap(received, "x")])
    return jnp.stack([across, swap(across, "c")])


def combine(partial):
    from_core = swap(partial[1], "c")
    chip_sum = partial[0].astype(jnp.float32) + from_core.astype(jnp.float32)
    from_x = swap(chip_sum[1].astype(jnp.bfloat16), "x")
    total = (chip_sum[0] + from_x.astype(jnp.float32)).astype(jnp.bfloat16)
    return lax.all_to_all(total, "z", 0, 0, tiled=True)


def body(
    fwd_input,
    fwd_experts,
    fwd_gates,
    bwd_input,
    bwd_grad,
    bwd_experts,
    bwd_gates,
    gate_proj,
    up_proj,
    down_proj,
):
    experts = lax.axis_size("z")
    tokens = fwd_input.shape[1]
    width = fwd_input.shape[2]
    capacity = min(tokens, 3 * tokens * TOPK // (2 * experts))
    w_gate = gate_proj[0]
    w_up = up_proj[0]
    w_down = down_proj[0]
    f_select, f_weights = routing(fwd_experts[0], fwd_gates[0], experts, capacity)
    b_select, b_weights = routing(bwd_experts[0], bwd_gates[0], experts, capacity)
    f_slots = into_slots(f_select, fwd_input[0]).reshape(experts, capacity, width)
    b_joined = jnp.concatenate([bwd_input[0], bwd_grad[0]], axis=1)
    b_slots = into_slots(b_select, b_joined).reshape(experts, capacity, 2 * width)
    f_rows = dispatch(f_slots)
    b_rows = dispatch(b_slots)
    f_partial = forward_rows(f_rows.reshape(-1, width), w_gate, w_up, w_down)
    b_partial = backward_rows(b_rows.reshape(-1, 2 * width), w_gate, w_up, w_down)
    f_out = combine(f_partial.reshape(2, 2, experts, capacity, width))
    b_out = combine(b_partial.reshape(2, 2, experts, capacity, width))
    high = lax.Precision.HIGHEST
    f_mixed = jnp.dot(
        f_weights, f_out.reshape(experts * capacity, width).astype(jnp.float32), precision=high
    )
    f_result = (fwd_input[0].astype(jnp.float32) + f_mixed).astype(jnp.bfloat16)
    b_mixed = jnp.dot(
        b_weights, b_out.reshape(experts * capacity, width).astype(jnp.float32), precision=high
    )
    b_result = (bwd_grad[0].astype(jnp.float32) + b_mixed).astype(jnp.bfloat16)
    next_section_input = passed_along(f_result[None], "pp", 1)
    prev_section_grad = passed_along(b_result[None], "pp", -1)
    return (next_section_input, prev_section_grad)


def solution(mesh):
    sections = mesh.shape["pp"]
    devices = mesh.shape["ep"]
    grid = mesh.devices.reshape(sections, devices // GROUP, 2, 2)
    split = Mesh(grid, ("pp",) + EP)
    rows = P("pp", EP, None)
    columns = P("pp", None, EP)
    in_specs = (rows, rows, rows, rows, rows, rows, rows, columns, columns, rows)
    out_specs = (rows, rows)
    return jax.shard_map(body, mesh=split, in_specs=in_specs, out_specs=out_specs, check_vma=False)
```

```python
import jax
import jax.numpy as jnp
from jax import lax
from jax.sharding import Mesh
from jax.sharding import PartitionSpec as P

GROUP = 4
TOPK = 2
EP = ("z", "x", "c")


def swap(value, axis):
    return lax.ppermute(value, axis, [(0, 1), (1, 0)])


def passed_along(value, axis, steps):
    count = lax.axis_size(axis)
    pairs = [(source, (source + steps) % count) for source in range(count)]
    return lax.ppermute(value, axis, pairs)


def routing(ids, gates, experts, capacity):
    pairs = ids.reshape(-1)
    hot = (pairs[:, None] == jnp.arange(experts, dtype=jnp.int32)[None, :]).astype(jnp.int32)
    before = jnp.cumsum(hot, axis=0) - hot
    slot = jnp.sum(hot * before, axis=1)
    target = (pairs * capacity + slot).reshape(ids.shape)
    columns = jnp.arange(experts * capacity, dtype=jnp.int32)
    match = (target[:, :, None] == columns[None, None, :]).astype(jnp.float32)
    select = jnp.sum(match, axis=1).astype(jnp.bfloat16)
    weights = jnp.sum(gates[:, :, None] * match, axis=1)
    return (select, weights)


def into_slots(select, rows_in):
    placed = lax.dot_general(
        select, rows_in, (((0,), (0,)), ((), ())), preferred_element_type=jnp.float32
    )
    return placed.astype(jnp.bfloat16)


def forward_rows(rows_in, w_gate, w_up, w_down):
    g = jnp.dot(rows_in, w_gate, preferred_element_type=jnp.float32)
    u = jnp.dot(rows_in, w_up, preferred_element_type=jnp.float32)
    hidden = (g * jax.nn.sigmoid(g) * u).astype(jnp.bfloat16)
    return jnp.dot(hidden, w_down, preferred_element_type=jnp.float32).astype(jnp.bfloat16)


def backward_rows(rows_all, w_gate, w_up, w_down):
    width = w_gate.shape[0]
    rows_in = rows_all[:, :width]
    rows_grad = rows_all[:, width:]
    g = jnp.dot(rows_in, w_gate, preferred_element_type=jnp.float32)
    u = jnp.dot(rows_in, w_up, preferred_element_type=jnp.float32)
    dh = lax.dot_general(
        rows_grad, w_down, (((1,), (1,)), ((), ())), preferred_element_type=jnp.float32
    )
    sig = jax.nn.sigmoid(g)
    grad_gate = (dh * u * sig * (1.0 + g * (1.0 - sig))).astype(jnp.bfloat16)
    grad_up = (dh * g * sig).astype(jnp.bfloat16)
    part = lax.dot_general(
        grad_gate, w_gate, (((1,), (1,)), ((), ())), preferred_element_type=jnp.float32
    )
    part = part + lax.dot_general(
        grad_up, w_up, (((1,), (1,)), ((), ())), preferred_element_type=jnp.float32
    )
    return part.astype(jnp.bfloat16)


def exchange(chunks):
    count = lax.axis_size("z")
    out = [chunks[0]]
    for d in range(1, count):
        pairs = [(i, i ^ d) for i in range(count)]
        out.append(lax.ppermute(chunks[d], "z", pairs))
    return jnp.stack(out)


def dispatch(slots):
    received = exchange(slots)
    across = jnp.stack([received, swap(received, "x")])
    return jnp.stack([across, swap(across, "c")])


def combine(partial):
    from_core = swap(partial[1], "c")
    chip_sum = partial[0].astype(jnp.float32) + from_core.astype(jnp.float32)
    from_x = swap(chip_sum[1].astype(jnp.bfloat16), "x")
    total = (chip_sum[0] + from_x.astype(jnp.float32)).astype(jnp.bfloat16)
    return exchange(total)


def body(
    fwd_input,
    fwd_experts,
    fwd_gates,
    bwd_input,
    bwd_grad,
    bwd_experts,
    bwd_gates,
    gate_proj,
    up_proj,
    down_proj,
):
    experts = lax.axis_size("z")
    tokens = fwd_input.shape[1]
    width = fwd_input.shape[2]
    capacity = min(tokens, 3 * tokens * TOPK // (2 * experts))
    w_gate = gate_proj[0]
    w_up = up_proj[0]
    w_down = down_proj[0]
    here = lax.axis_index("z")
    f_select, f_weights = routing(fwd_experts[0] ^ here, fwd_gates[0], experts, capacity)
    b_select, b_weights = routing(bwd_experts[0] ^ here, bwd_gates[0], experts, capacity)
    f_slots = into_slots(f_select, fwd_input[0]).reshape(experts, capacity, width)
    b_joined = jnp.concatenate([bwd_input[0], bwd_grad[0]], axis=1)
    b_slots = into_slots(b_select, b_joined).reshape(experts, capacity, 2 * width)
    f_rows = dispatch(f_slots)
    b_rows = dispatch(b_slots)
    f_partial = forward_rows(f_rows.reshape(-1, width), w_gate, w_up, w_down)
    b_partial = backward_rows(b_rows.reshape(-1, 2 * width), w_gate, w_up, w_down)
    f_out = combine(f_partial.reshape(2, 2, experts, capacity, width))
    b_out = combine(b_partial.reshape(2, 2, experts, capacity, width))
    high = lax.Precision.HIGHEST
    f_mixed = jnp.dot(
        f_weights, f_out.reshape(experts * capacity, width).astype(jnp.float32), precision=high
    )
    f_result = (fwd_input[0].astype(jnp.float32) + f_mixed).astype(jnp.bfloat16)
    b_mixed = jnp.dot(
        b_weights, b_out.reshape(experts * capacity, width).astype(jnp.float32), precision=high
    )
    b_result = (bwd_grad[0].astype(jnp.float32) + b_mixed).astype(jnp.bfloat16)
    next_section_input = passed_along(f_result[None], "pp", 1)
    prev_section_grad = passed_along(b_result[None], "pp", -1)
    return (next_section_input, prev_section_grad)


def solution(mesh):
    sections = mesh.shape["pp"]
    devices = mesh.shape["ep"]
    grid = mesh.devices.reshape(sections, devices // GROUP, 2, 2)
    split = Mesh(grid, ("pp",) + EP)
    rows = P("pp", EP, None)
    columns = P("pp", None, EP)
    in_specs = (rows, rows, rows, rows, rows, rows, rows, columns, columns, rows)
    out_specs = (rows, rows)
    return jax.shard_map(body, mesh=split, in_specs=in_specs, out_specs=out_specs, check_vma=False)
```

```python
import jax
import jax.numpy as jnp
from jax import lax
from jax.sharding import Mesh
from jax.sharding import PartitionSpec as P

GROUP = 4
TOPK = 2
EP = ("z", "x", "c")


def swap(value, axis):
    return lax.ppermute(value, axis, [(0, 1), (1, 0)])


def passed_along(value, axis, steps):
    count = lax.axis_size(axis)
    pairs = [(source, (source + steps) % count) for source in range(count)]
    return lax.ppermute(value, axis, pairs)


def routing(ids, gates, experts, capacity):
    pairs = ids.reshape(-1)
    hot = (pairs[:, None] == jnp.arange(experts, dtype=jnp.int32)[None, :]).astype(jnp.int32)
    before = jnp.cumsum(hot, axis=0) - hot
    slot = jnp.sum(hot * before, axis=1)
    target = (pairs * capacity + slot).reshape(ids.shape)
    columns = jnp.arange(experts * capacity, dtype=jnp.int32)
    match = (target[:, :, None] == columns[None, None, :]).astype(jnp.float32)
    select = jnp.sum(match, axis=1).astype(jnp.bfloat16)
    weights = jnp.sum(gates[:, :, None] * match, axis=1)
    return (select, weights)


def into_slots(select, rows_in):
    placed = lax.dot_general(
        select, rows_in, (((0,), (0,)), ((), ())), preferred_element_type=jnp.float32
    )
    return placed.astype(jnp.bfloat16)


def forward_rows(rows_in, w_gate, w_up, w_down):
    g = jnp.dot(rows_in, w_gate, preferred_element_type=jnp.float32)
    u = jnp.dot(rows_in, w_up, preferred_element_type=jnp.float32)
    hidden = (g * jax.nn.sigmoid(g) * u).astype(jnp.bfloat16)
    return jnp.dot(hidden, w_down, preferred_element_type=jnp.float32).astype(jnp.bfloat16)


def backward_rows(rows_all, w_gate, w_up, w_down):
    width = w_gate.shape[0]
    rows_in = rows_all[:, :width]
    rows_grad = rows_all[:, width:]
    g = jnp.dot(rows_in, w_gate, preferred_element_type=jnp.float32)
    u = jnp.dot(rows_in, w_up, preferred_element_type=jnp.float32)
    dh = lax.dot_general(
        rows_grad, w_down, (((1,), (1,)), ((), ())), preferred_element_type=jnp.float32
    )
    sig = jax.nn.sigmoid(g)
    grad_gate = (dh * u * sig * (1.0 + g * (1.0 - sig))).astype(jnp.bfloat16)
    grad_up = (dh * g * sig).astype(jnp.bfloat16)
    part = lax.dot_general(
        grad_gate, w_gate, (((1,), (1,)), ((), ())), preferred_element_type=jnp.float32
    )
    part = part + lax.dot_general(
        grad_up, w_up, (((1,), (1,)), ((), ())), preferred_element_type=jnp.float32
    )
    return part.astype(jnp.bfloat16)


def exchange(chunks):
    count = lax.axis_size("z")
    out = [chunks[0]]
    for d in range(1, count):
        pairs = [(i, i ^ d) for i in range(count)]
        out.append(lax.ppermute(chunks[d], "z", pairs))
    return jnp.stack(out)


def dispatch(slots):
    received = exchange(slots)
    across = jnp.stack([received, swap(received, "x")])
    return jnp.stack([across, swap(across, "c")])


def combine(partial):
    from_core = swap(partial[1], "c")
    chip_sum = partial[0].astype(jnp.float32) + from_core.astype(jnp.float32)
    from_x = swap(chip_sum[1].astype(jnp.bfloat16), "x")
    total = (chip_sum[0] + from_x.astype(jnp.float32)).astype(jnp.bfloat16)
    return exchange(total)


def body(
    fwd_input,
    fwd_experts,
    fwd_gates,
    bwd_input,
    bwd_grad,
    bwd_experts,
    bwd_gates,
    gate_proj,
    up_proj,
    down_proj,
):
    experts = lax.axis_size("z")
    tokens = fwd_input.shape[1]
    width = fwd_input.shape[2]
    capacity = min(tokens, 3 * tokens * TOPK // (2 * experts))
    w_gate = gate_proj[0]
    w_up = up_proj[0]
    w_down = down_proj[0]
    here = lax.axis_index("z")
    f_select, f_weights = routing(fwd_experts[0] ^ here, fwd_gates[0], experts, capacity)
    b_select, b_weights = routing(bwd_experts[0] ^ here, bwd_gates[0], experts, capacity)
    f_slots = into_slots(f_select, fwd_input[0]).reshape(experts, capacity, width)
    b_joined = jnp.concatenate([bwd_input[0], bwd_grad[0]], axis=1)
    b_slots = into_slots(b_select, b_joined).reshape(experts, capacity, 2 * width)
    half = capacity // 2
    f_outs, b_outs = [], []
    for part in range(2):
        window = slice(part * half, (part + 1) * half)
        b_rows = dispatch(b_slots[:, window])
        f_rows = dispatch(f_slots[:, window])
        b_partial = backward_rows(b_rows.reshape(-1, 2 * width), w_gate, w_up, w_down)
        f_partial = forward_rows(f_rows.reshape(-1, width), w_gate, w_up, w_down)
        b_outs.append(combine(b_partial.reshape(2, 2, experts, half, width)))
        f_outs.append(combine(f_partial.reshape(2, 2, experts, half, width)))
    f_out = jnp.concatenate(f_outs, axis=1)
    b_out = jnp.concatenate(b_outs, axis=1)
    high = lax.Precision.HIGHEST
    f_mixed = jnp.dot(
        f_weights, f_out.reshape(experts * capacity, width).astype(jnp.float32), precision=high
    )
    f_result = (fwd_input[0].astype(jnp.float32) + f_mixed).astype(jnp.bfloat16)
    b_mixed = jnp.dot(
        b_weights, b_out.reshape(experts * capacity, width).astype(jnp.float32), precision=high
    )
    b_result = (bwd_grad[0].astype(jnp.float32) + b_mixed).astype(jnp.bfloat16)
    next_section_input = passed_along(f_result[None], "pp", 1)
    prev_section_grad = passed_along(b_result[None], "pp", -1)
    return (next_section_input, prev_section_grad)


def solution(mesh):
    sections = mesh.shape["pp"]
    devices = mesh.shape["ep"]
    grid = mesh.devices.reshape(sections, devices // GROUP, 2, 2)
    split = Mesh(grid, ("pp",) + EP)
    rows = P("pp", EP, None)
    columns = P("pp", None, EP)
    in_specs = (rows, rows, rows, rows, rows, rows, rows, columns, columns, rows)
    out_specs = (rows, rows)
    return jax.shard_map(body, mesh=split, in_specs=in_specs, out_specs=out_specs, check_vma=False)
```

```python
import jax
import jax.numpy as jnp
from jax import lax
from jax.sharding import Mesh
from jax.sharding import PartitionSpec as P

GROUP = 4
TOPK = 2
EP = ("z", "x", "c")


def swap(value, axis):
    return lax.ppermute(value, axis, [(0, 1), (1, 0)])


def passed_along(value, axis, steps):
    count = lax.axis_size(axis)
    pairs = [(source, (source + steps) % count) for source in range(count)]
    return lax.ppermute(value, axis, pairs)


def routing(ids, gates, experts, capacity):
    pairs = ids.reshape(-1)
    hot = (pairs[:, None] == jnp.arange(experts, dtype=jnp.int32)[None, :]).astype(jnp.int32)
    before = jnp.cumsum(hot, axis=0) - hot
    slot = jnp.sum(hot * before, axis=1)
    target = (pairs * capacity + slot).reshape(ids.shape)
    columns = jnp.arange(experts * capacity, dtype=jnp.int32)
    match = (target[:, :, None] == columns[None, None, :]).astype(jnp.float32)
    select = jnp.sum(match, axis=1).astype(jnp.bfloat16)
    weights = jnp.sum(gates[:, :, None] * match, axis=1)
    return (select, weights)


def into_slots(select, rows_in):
    placed = lax.dot_general(
        select, rows_in, (((0,), (0,)), ((), ())), preferred_element_type=jnp.float32
    )
    return placed.astype(jnp.bfloat16)


def forward_rows(rows_in, w_gate, w_up, w_down):
    g = jnp.dot(rows_in, w_gate, preferred_element_type=jnp.float32)
    u = jnp.dot(rows_in, w_up, preferred_element_type=jnp.float32)
    hidden = (g * jax.nn.sigmoid(g) * u).astype(jnp.bfloat16)
    return jnp.dot(hidden, w_down, preferred_element_type=jnp.float32).astype(jnp.bfloat16)


def backward_rows(rows_all, w_gate, w_up, w_down):
    width = w_gate.shape[0]
    rows_in = rows_all[:, :width]
    rows_grad = rows_all[:, width:]
    g = jnp.dot(rows_in, w_gate, preferred_element_type=jnp.float32)
    u = jnp.dot(rows_in, w_up, preferred_element_type=jnp.float32)
    dh = lax.dot_general(
        rows_grad, w_down, (((1,), (1,)), ((), ())), preferred_element_type=jnp.float32
    )
    sig = jax.nn.sigmoid(g)
    grad_gate = (dh * u * sig * (1.0 + g * (1.0 - sig))).astype(jnp.bfloat16)
    grad_up = (dh * g * sig).astype(jnp.bfloat16)
    part = lax.dot_general(
        grad_gate, w_gate, (((1,), (1,)), ((), ())), preferred_element_type=jnp.float32
    )
    part = part + lax.dot_general(
        grad_up, w_up, (((1,), (1,)), ((), ())), preferred_element_type=jnp.float32
    )
    return part.astype(jnp.bfloat16)


def exchange(chunks):
    count = lax.axis_size("z")
    out = [chunks[0]]
    for d in range(1, count):
        pairs = [(i, i ^ d) for i in range(count)]
        out.append(lax.ppermute(chunks[d], "z", pairs))
    return jnp.stack(out)


def dispatch(slots):
    count = lax.axis_size("z")
    pieces = []
    for d in range(count):
        if d == 0:
            received = slots[0]
        else:
            received = lax.ppermute(slots[d], "z", [(i, i ^ d) for i in range(count)])
        across = jnp.stack([received, swap(received, "x")])
        pieces.append(jnp.stack([across, swap(across, "c")]))
    return jnp.stack(pieces, axis=2)


def combine(partial):
    from_core = swap(partial[1], "c")
    chip_sum = partial[0].astype(jnp.float32) + from_core.astype(jnp.float32)
    from_x = swap(chip_sum[1].astype(jnp.bfloat16), "x")
    total = (chip_sum[0] + from_x.astype(jnp.float32)).astype(jnp.bfloat16)
    return exchange(total)


def body(
    fwd_input,
    fwd_experts,
    fwd_gates,
    bwd_input,
    bwd_grad,
    bwd_experts,
    bwd_gates,
    gate_proj,
    up_proj,
    down_proj,
):
    experts = lax.axis_size("z")
    tokens = fwd_input.shape[1]
    width = fwd_input.shape[2]
    capacity = min(tokens, 3 * tokens * TOPK // (2 * experts))
    w_gate = gate_proj[0]
    w_up = up_proj[0]
    w_down = down_proj[0]
    here = lax.axis_index("z")
    f_select, f_weights = routing(fwd_experts[0] ^ here, fwd_gates[0], experts, capacity)
    b_select, b_weights = routing(bwd_experts[0] ^ here, bwd_gates[0], experts, capacity)
    f_slots = into_slots(f_select, fwd_input[0]).reshape(experts, capacity, width)
    b_joined = jnp.concatenate([bwd_input[0], bwd_grad[0]], axis=1)
    b_slots = into_slots(b_select, b_joined).reshape(experts, capacity, 2 * width)
    f_rows = dispatch(f_slots)
    b_rows = dispatch(b_slots)
    f_partial = forward_rows(f_rows.reshape(-1, width), w_gate, w_up, w_down)
    b_partial = backward_rows(b_rows.reshape(-1, 2 * width), w_gate, w_up, w_down)
    f_out = combine(f_partial.reshape(2, 2, experts, capacity, width))
    b_out = combine(b_partial.reshape(2, 2, experts, capacity, width))
    high = lax.Precision.HIGHEST
    f_mixed = jnp.dot(
        f_weights, f_out.reshape(experts * capacity, width).astype(jnp.float32), precision=high
    )
    f_result = (fwd_input[0].astype(jnp.float32) + f_mixed).astype(jnp.bfloat16)
    b_mixed = jnp.dot(
        b_weights, b_out.reshape(experts * capacity, width).astype(jnp.float32), precision=high
    )
    b_result = (bwd_grad[0].astype(jnp.float32) + b_mixed).astype(jnp.bfloat16)
    next_section_input = passed_along(f_result[None], "pp", 1)
    prev_section_grad = passed_along(b_result[None], "pp", -1)
    return (next_section_input, prev_section_grad)


def solution(mesh):
    sections = mesh.shape["pp"]
    devices = mesh.shape["ep"]
    grid = mesh.devices.reshape(sections, devices // GROUP, 2, 2)
    split = Mesh(grid, ("pp",) + EP)
    rows = P("pp", EP, None)
    columns = P("pp", None, EP)
    in_specs = (rows, rows, rows, rows, rows, rows, rows, columns, columns, rows)
    out_specs = (rows, rows)
    return jax.shard_map(body, mesh=split, in_specs=in_specs, out_specs=out_specs, check_vma=False)
```

```python
import jax
import jax.numpy as jnp
from jax import lax
from jax.sharding import Mesh
from jax.sharding import PartitionSpec as P

GROUP = 4
TOPK = 2
EP = ("z", "x", "c")


def swap(value, axis):
    return lax.ppermute(value, axis, [(0, 1), (1, 0)])


def passed_along(value, axis, steps):
    count = lax.axis_size(axis)
    pairs = [(source, (source + steps) % count) for source in range(count)]
    return lax.ppermute(value, axis, pairs)


def routing(ids, gates, experts, capacity):
    pairs = ids.reshape(-1)
    hot = (pairs[:, None] == jnp.arange(experts, dtype=jnp.int32)[None, :]).astype(jnp.int32)
    before = jnp.cumsum(hot, axis=0) - hot
    slot = jnp.sum(hot * before, axis=1)
    target = (pairs * capacity + slot).reshape(ids.shape)
    columns = jnp.arange(experts * capacity, dtype=jnp.int32)
    match = (target[:, :, None] == columns[None, None, :]).astype(jnp.float32)
    select = jnp.sum(match, axis=1).astype(jnp.bfloat16)
    weights = jnp.sum(gates[:, :, None] * match, axis=1)
    return (select, weights)


def into_slots(select, rows_in):
    placed = lax.dot_general(
        select, rows_in, (((0,), (0,)), ((), ())), preferred_element_type=jnp.float32
    )
    return placed.astype(jnp.bfloat16)


def forward_rows(rows_in, w_gate, w_up, w_down):
    g = jnp.dot(rows_in, w_gate, preferred_element_type=jnp.float32)
    u = jnp.dot(rows_in, w_up, preferred_element_type=jnp.float32)
    hidden = (g * jax.nn.sigmoid(g) * u).astype(jnp.bfloat16)
    return jnp.dot(hidden, w_down, preferred_element_type=jnp.float32).astype(jnp.bfloat16)


def backward_rows(rows_all, w_gate, w_up, w_down):
    width = w_gate.shape[0]
    rows_in = rows_all[:, :width]
    rows_grad = rows_all[:, width:]
    g = jnp.dot(rows_in, w_gate, preferred_element_type=jnp.float32)
    u = jnp.dot(rows_in, w_up, preferred_element_type=jnp.float32)
    dh = lax.dot_general(
        rows_grad, w_down, (((1,), (1,)), ((), ())), preferred_element_type=jnp.float32
    )
    sig = jax.nn.sigmoid(g)
    grad_gate = (dh * u * sig * (1.0 + g * (1.0 - sig))).astype(jnp.bfloat16)
    grad_up = (dh * g * sig).astype(jnp.bfloat16)
    part = lax.dot_general(
        grad_gate, w_gate, (((1,), (1,)), ((), ())), preferred_element_type=jnp.float32
    )
    part = part + lax.dot_general(
        grad_up, w_up, (((1,), (1,)), ((), ())), preferred_element_type=jnp.float32
    )
    return part.astype(jnp.bfloat16)


def to_group(chunk, d):
    count = lax.axis_size("z")
    received = chunk if d == 0 else lax.ppermute(chunk, "z", [(i, i ^ d) for i in range(count)])
    across = jnp.stack([received, swap(received, "x")])
    return jnp.stack([across, swap(across, "c")])


def from_group(partial, d):
    count = lax.axis_size("z")
    from_core = swap(partial[1], "c")
    chip_sum = partial[0].astype(jnp.float32) + from_core.astype(jnp.float32)
    from_x = swap(chip_sum[1].astype(jnp.bfloat16), "x")
    total = (chip_sum[0] + from_x.astype(jnp.float32)).astype(jnp.bfloat16)
    if d == 0:
        return total
    return lax.ppermute(total, "z", [(i, i ^ d) for i in range(count)])


def body(
    fwd_input,
    fwd_experts,
    fwd_gates,
    bwd_input,
    bwd_grad,
    bwd_experts,
    bwd_gates,
    gate_proj,
    up_proj,
    down_proj,
):
    experts = lax.axis_size("z")
    tokens = fwd_input.shape[1]
    width = fwd_input.shape[2]
    capacity = min(tokens, 3 * tokens * TOPK // (2 * experts))
    w_gate = gate_proj[0]
    w_up = up_proj[0]
    w_down = down_proj[0]
    here = lax.axis_index("z")
    f_select, f_weights = routing(fwd_experts[0] ^ here, fwd_gates[0], experts, capacity)
    b_select, b_weights = routing(bwd_experts[0] ^ here, bwd_gates[0], experts, capacity)
    f_slots = into_slots(f_select, fwd_input[0]).reshape(experts, capacity, width)
    b_joined = jnp.concatenate([bwd_input[0], bwd_grad[0]], axis=1)
    b_slots = into_slots(b_select, b_joined).reshape(experts, capacity, 2 * width)
    f_outs, b_outs = [], []
    for d in range(experts):
        f_rows = to_group(f_slots[d], d)
        b_rows = to_group(b_slots[d], d)
        f_partial = forward_rows(f_rows.reshape(-1, width), w_gate, w_up, w_down)
        b_partial = backward_rows(b_rows.reshape(-1, 2 * width), w_gate, w_up, w_down)
        f_outs.append(from_group(f_partial.reshape(2, 2, capacity, width), d))
        b_outs.append(from_group(b_partial.reshape(2, 2, capacity, width), d))
    f_out = jnp.stack(f_outs)
    b_out = jnp.stack(b_outs)
    high = lax.Precision.HIGHEST
    f_mixed = jnp.dot(
        f_weights, f_out.reshape(experts * capacity, width).astype(jnp.float32), precision=high
    )
    f_result = (fwd_input[0].astype(jnp.float32) + f_mixed).astype(jnp.bfloat16)
    b_mixed = jnp.dot(
        b_weights, b_out.reshape(experts * capacity, width).astype(jnp.float32), precision=high
    )
    b_result = (bwd_grad[0].astype(jnp.float32) + b_mixed).astype(jnp.bfloat16)
    next_section_input = passed_along(f_result[None], "pp", 1)
    prev_section_grad = passed_along(b_result[None], "pp", -1)
    return (next_section_input, prev_section_grad)


def solution(mesh):
    sections = mesh.shape["pp"]
    devices = mesh.shape["ep"]
    grid = mesh.devices.reshape(sections, devices // GROUP, 2, 2)
    split = Mesh(grid, ("pp",) + EP)
    rows = P("pp", EP, None)
    columns = P("pp", None, EP)
    in_specs = (rows, rows, rows, rows, rows, rows, rows, columns, columns, rows)
    out_specs = (rows, rows)
    return jax.shard_map(body, mesh=split, in_specs=in_specs, out_specs=out_specs, check_vma=False)
```

```python
import jax
import jax.numpy as jnp
from jax import lax
from jax.sharding import Mesh
from jax.sharding import PartitionSpec as P

GROUP = 4
TOPK = 2
EP = ("z", "x", "c")


def swap(value, axis):
    return lax.ppermute(value, axis, [(0, 1), (1, 0)])


def passed_along(value, axis, steps):
    count = lax.axis_size(axis)
    pairs = [(source, (source + steps) % count) for source in range(count)]
    return lax.ppermute(value, axis, pairs)


def routing(ids, gates, experts, capacity):
    pairs = ids.reshape(-1)
    hot = (pairs[:, None] == jnp.arange(experts, dtype=jnp.int32)[None, :]).astype(jnp.int32)
    before = jnp.cumsum(hot, axis=0) - hot
    slot = jnp.sum(hot * before, axis=1)
    target = (pairs * capacity + slot).reshape(ids.shape)
    columns = jnp.arange(experts * capacity, dtype=jnp.int32)
    match = (target[:, :, None] == columns[None, None, :]).astype(jnp.float32)
    select = jnp.sum(match, axis=1).astype(jnp.bfloat16)
    weights = jnp.sum(gates[:, :, None] * match, axis=1)
    return (select, weights)


def into_slots(select, rows_in):
    placed = lax.dot_general(
        select, rows_in, (((0,), (0,)), ((), ())), preferred_element_type=jnp.float32
    )
    return placed.astype(jnp.bfloat16)


def forward_rows(rows_in, w_gate, w_up, w_down):
    g = jnp.dot(rows_in, w_gate, preferred_element_type=jnp.float32)
    u = jnp.dot(rows_in, w_up, preferred_element_type=jnp.float32)
    hidden = (g * jax.nn.sigmoid(g) * u).astype(jnp.bfloat16)
    return jnp.dot(hidden, w_down, preferred_element_type=jnp.float32).astype(jnp.bfloat16)


def backward_rows(rows_all, w_gate, w_up, w_down):
    width = w_gate.shape[0]
    rows_in = rows_all[:, :width]
    rows_grad = rows_all[:, width:]
    g = jnp.dot(rows_in, w_gate, preferred_element_type=jnp.float32)
    u = jnp.dot(rows_in, w_up, preferred_element_type=jnp.float32)
    dh = lax.dot_general(
        rows_grad, w_down, (((1,), (1,)), ((), ())), preferred_element_type=jnp.float32
    )
    sig = jax.nn.sigmoid(g)
    grad_gate = (dh * u * sig * (1.0 + g * (1.0 - sig))).astype(jnp.bfloat16)
    grad_up = (dh * g * sig).astype(jnp.bfloat16)
    part = lax.dot_general(
        grad_gate, w_gate, (((1,), (1,)), ((), ())), preferred_element_type=jnp.float32
    )
    part = part + lax.dot_general(
        grad_up, w_up, (((1,), (1,)), ((), ())), preferred_element_type=jnp.float32
    )
    return part.astype(jnp.bfloat16)


def dispatch(slots):
    count = lax.axis_size("z")
    pieces = []
    for d in range(count):
        if d == 0:
            received = slots[0]
        else:
            received = lax.ppermute(slots[d], "z", [(i, i ^ d) for i in range(count)])
        across = jnp.stack([received, swap(received, "x")])
        pieces.append(jnp.stack([across, swap(across, "c")]))
    return jnp.stack(pieces, axis=2)


def reduce_group(partial):
    from_core = swap(partial[1], "c")
    chip_sum = partial[0].astype(jnp.float32) + from_core.astype(jnp.float32)
    totals = []
    for d in range(chip_sum.shape[1]):
        from_x = swap(chip_sum[1, d].astype(jnp.bfloat16), "x")
        totals.append((chip_sum[0, d] + from_x.astype(jnp.float32)).astype(jnp.bfloat16))
    return totals


def returned(totals):
    count = lax.axis_size("z")
    out = [totals[0]]
    for d in range(1, count):
        out.append(lax.ppermute(totals[d], "z", [(i, i ^ d) for i in range(count)]))
    return jnp.stack(out)


def body(
    fwd_input,
    fwd_experts,
    fwd_gates,
    bwd_input,
    bwd_grad,
    bwd_experts,
    bwd_gates,
    gate_proj,
    up_proj,
    down_proj,
):
    experts = lax.axis_size("z")
    tokens = fwd_input.shape[1]
    width = fwd_input.shape[2]
    capacity = min(tokens, 3 * tokens * TOPK // (2 * experts))
    w_gate = gate_proj[0]
    w_up = up_proj[0]
    w_down = down_proj[0]
    here = lax.axis_index("z")
    f_select, f_weights = routing(fwd_experts[0] ^ here, fwd_gates[0], experts, capacity)
    b_select, b_weights = routing(bwd_experts[0] ^ here, bwd_gates[0], experts, capacity)
    f_slots = into_slots(f_select, fwd_input[0]).reshape(experts, capacity, width)
    b_joined = jnp.concatenate([bwd_input[0], bwd_grad[0]], axis=1)
    b_slots = into_slots(b_select, b_joined).reshape(experts, capacity, 2 * width)
    f_rows = dispatch(f_slots)
    b_rows = dispatch(b_slots)
    f_partial = forward_rows(f_rows.reshape(-1, width), w_gate, w_up, w_down)
    f_totals = reduce_group(f_partial.reshape(2, 2, experts, capacity, width))
    b_rows, f_totals = lax.optimization_barrier((b_rows, f_totals))
    f_out = returned(f_totals)
    b_partial = backward_rows(b_rows.reshape(-1, 2 * width), w_gate, w_up, w_down)
    b_out = returned(reduce_group(b_partial.reshape(2, 2, experts, capacity, width)))
    high = lax.Precision.HIGHEST
    f_mixed = jnp.dot(
        f_weights, f_out.reshape(experts * capacity, width).astype(jnp.float32), precision=high
    )
    f_result = (fwd_input[0].astype(jnp.float32) + f_mixed).astype(jnp.bfloat16)
    b_mixed = jnp.dot(
        b_weights, b_out.reshape(experts * capacity, width).astype(jnp.float32), precision=high
    )
    b_result = (bwd_grad[0].astype(jnp.float32) + b_mixed).astype(jnp.bfloat16)
    next_section_input = passed_along(f_result[None], "pp", 1)
    prev_section_grad = passed_along(b_result[None], "pp", -1)
    return (next_section_input, prev_section_grad)


def solution(mesh):
    sections = mesh.shape["pp"]
    devices = mesh.shape["ep"]
    grid = mesh.devices.reshape(sections, devices // GROUP, 2, 2)
    split = Mesh(grid, ("pp",) + EP)
    rows = P("pp", EP, None)
    columns = P("pp", None, EP)
    in_specs = (rows, rows, rows, rows, rows, rows, rows, columns, columns, rows)
    out_specs = (rows, rows)
    return jax.shard_map(body, mesh=split, in_specs=in_specs, out_specs=out_specs, check_vma=False)
```

```python
import jax
import jax.numpy as jnp
from jax import lax
from jax.sharding import Mesh
from jax.sharding import PartitionSpec as P

GROUP = 4
TOPK = 2
EP = ("z", "x", "c")


def swap(value, axis):
    return lax.ppermute(value, axis, [(0, 1), (1, 0)])


def passed_along(value, axis, steps):
    count = lax.axis_size(axis)
    pairs = [(source, (source + steps) % count) for source in range(count)]
    return lax.ppermute(value, axis, pairs)


def routing(ids, gates, experts, capacity):
    pairs = ids.reshape(-1)
    hot = (pairs[:, None] == jnp.arange(experts, dtype=jnp.int32)[None, :]).astype(jnp.int32)
    before = jnp.cumsum(hot, axis=0) - hot
    slot = jnp.sum(hot * before, axis=1)
    target = (pairs * capacity + slot).reshape(ids.shape)
    columns = jnp.arange(experts * capacity, dtype=jnp.int32)
    match = (target[:, :, None] == columns[None, None, :]).astype(jnp.float32)
    select = jnp.sum(match, axis=1).astype(jnp.bfloat16)
    weights = jnp.sum(gates[:, :, None] * match, axis=1)
    return (select, weights)


def into_slots(select, rows_in):
    placed = lax.dot_general(
        select, rows_in, (((0,), (0,)), ((), ())), preferred_element_type=jnp.float32
    )
    return placed.astype(jnp.bfloat16)


def forward_rows(rows_in, w_gate, w_up, w_down):
    g = jnp.dot(rows_in, w_gate, preferred_element_type=jnp.float32)
    u = jnp.dot(rows_in, w_up, preferred_element_type=jnp.float32)
    hidden = (g * jax.nn.sigmoid(g) * u).astype(jnp.bfloat16)
    return jnp.dot(hidden, w_down, preferred_element_type=jnp.float32).astype(jnp.bfloat16)


def backward_rows(rows_all, w_gate, w_up, w_down):
    width = w_gate.shape[0]
    rows_in = rows_all[:, :width]
    rows_grad = rows_all[:, width:]
    g = jnp.dot(rows_in, w_gate, preferred_element_type=jnp.float32)
    u = jnp.dot(rows_in, w_up, preferred_element_type=jnp.float32)
    dh = lax.dot_general(
        rows_grad, w_down, (((1,), (1,)), ((), ())), preferred_element_type=jnp.float32
    )
    sig = jax.nn.sigmoid(g)
    grad_gate = (dh * u * sig * (1.0 + g * (1.0 - sig))).astype(jnp.bfloat16)
    grad_up = (dh * g * sig).astype(jnp.bfloat16)
    part = lax.dot_general(
        grad_gate, w_gate, (((1,), (1,)), ((), ())), preferred_element_type=jnp.float32
    )
    part = part + lax.dot_general(
        grad_up, w_up, (((1,), (1,)), ((), ())), preferred_element_type=jnp.float32
    )
    return part.astype(jnp.bfloat16)


def dispatch(slots):
    count = lax.axis_size("z")
    pieces = []
    for d in range(count):
        if d == 0:
            received = slots[0]
        else:
            received = lax.ppermute(slots[d], "z", [(i, i ^ d) for i in range(count)])
        across = jnp.stack([received, swap(received, "x")])
        pieces.append(jnp.stack([across, swap(across, "c")]))
    return jnp.stack(pieces, axis=2)


def reduce_group(partial):
    count = partial.shape[2]
    totals = [None] * count
    for d in list(range(1, count)) + [0]:
        from_core = swap(partial[1, :, d], "c")
        chip_sum = partial[0, :, d].astype(jnp.float32) + from_core.astype(jnp.float32)
        from_x = swap(chip_sum[1].astype(jnp.bfloat16), "x")
        totals[d] = (chip_sum[0] + from_x.astype(jnp.float32)).astype(jnp.bfloat16)
    return totals


def returned(totals):
    count = lax.axis_size("z")
    out = [totals[0]]
    for d in range(1, count):
        out.append(lax.ppermute(totals[d], "z", [(i, i ^ d) for i in range(count)]))
    return jnp.stack(out)


def body(
    fwd_input,
    fwd_experts,
    fwd_gates,
    bwd_input,
    bwd_grad,
    bwd_experts,
    bwd_gates,
    gate_proj,
    up_proj,
    down_proj,
):
    experts = lax.axis_size("z")
    tokens = fwd_input.shape[1]
    width = fwd_input.shape[2]
    capacity = min(tokens, 3 * tokens * TOPK // (2 * experts))
    w_gate = gate_proj[0]
    w_up = up_proj[0]
    w_down = down_proj[0]
    here = lax.axis_index("z")
    f_select, f_weights = routing(fwd_experts[0] ^ here, fwd_gates[0], experts, capacity)
    b_select, b_weights = routing(bwd_experts[0] ^ here, bwd_gates[0], experts, capacity)
    f_slots = into_slots(f_select, fwd_input[0]).reshape(experts, capacity, width)
    b_joined = jnp.concatenate([bwd_input[0], bwd_grad[0]], axis=1)
    b_slots = into_slots(b_select, b_joined).reshape(experts, capacity, 2 * width)
    f_rows = dispatch(f_slots)
    b_rows = dispatch(b_slots)
    f_partial = forward_rows(f_rows.reshape(-1, width), w_gate, w_up, w_down)
    f_totals = reduce_group(f_partial.reshape(2, 2, experts, capacity, width))
    b_rows, f_totals = lax.optimization_barrier((b_rows, f_totals))
    f_out = returned(f_totals)
    b_partial = backward_rows(b_rows.reshape(-1, 2 * width), w_gate, w_up, w_down)
    b_out = returned(reduce_group(b_partial.reshape(2, 2, experts, capacity, width)))
    high = lax.Precision.HIGHEST
    f_mixed = jnp.dot(
        f_weights, f_out.reshape(experts * capacity, width).astype(jnp.float32), precision=high
    )
    f_result = (fwd_input[0].astype(jnp.float32) + f_mixed).astype(jnp.bfloat16)
    b_mixed = jnp.dot(
        b_weights, b_out.reshape(experts * capacity, width).astype(jnp.float32), precision=high
    )
    b_result = (bwd_grad[0].astype(jnp.float32) + b_mixed).astype(jnp.bfloat16)
    next_section_input = passed_along(f_result[None], "pp", 1)
    prev_section_grad = passed_along(b_result[None], "pp", -1)
    return (next_section_input, prev_section_grad)


def solution(mesh):
    sections = mesh.shape["pp"]
    devices = mesh.shape["ep"]
    grid = mesh.devices.reshape(sections, devices // GROUP, 2, 2)
    split = Mesh(grid, ("pp",) + EP)
    rows = P("pp", EP, None)
    columns = P("pp", None, EP)
    in_specs = (rows, rows, rows, rows, rows, rows, rows, columns, columns, rows)
    out_specs = (rows, rows)
    return jax.shard_map(body, mesh=split, in_specs=in_specs, out_specs=out_specs, check_vma=False)
```

```python
import jax
import jax.numpy as jnp
from jax import lax
from jax.sharding import Mesh
from jax.sharding import PartitionSpec as P

GROUP = 4
TOPK = 2
EP = ("z", "x", "c")


def swap(value, axis):
    return lax.ppermute(value, axis, [(0, 1), (1, 0)])


def passed_along(value, axis, steps):
    count = lax.axis_size(axis)
    pairs = [(source, (source + steps) % count) for source in range(count)]
    return lax.ppermute(value, axis, pairs)


def routing(ids, gates, experts, capacity):
    pairs = ids.reshape(-1)
    hot = (pairs[:, None] == jnp.arange(experts, dtype=jnp.int32)[None, :]).astype(jnp.int32)
    before = jnp.cumsum(hot, axis=0) - hot
    slot = jnp.sum(hot * before, axis=1)
    target = (pairs * capacity + slot).reshape(ids.shape)
    columns = jnp.arange(experts * capacity, dtype=jnp.int32)
    match = (target[:, :, None] == columns[None, None, :]).astype(jnp.float32)
    select = jnp.sum(match, axis=1).astype(jnp.bfloat16)
    weights = jnp.sum(gates[:, :, None] * match, axis=1)
    return (select, weights)


def into_slots(select, rows_in):
    placed = lax.dot_general(
        select, rows_in, (((0,), (0,)), ((), ())), preferred_element_type=jnp.float32
    )
    return placed.astype(jnp.bfloat16)


def forward_rows(rows_in, w_gate, w_up, w_down):
    g = jnp.dot(rows_in, w_gate, preferred_element_type=jnp.float32)
    u = jnp.dot(rows_in, w_up, preferred_element_type=jnp.float32)
    hidden = (g * jax.nn.sigmoid(g) * u).astype(jnp.bfloat16)
    return jnp.dot(hidden, w_down, preferred_element_type=jnp.float32).astype(jnp.bfloat16)


def backward_rows(rows_all, w_gate, w_up, w_down):
    width = w_gate.shape[0]
    rows_in = rows_all[:, :width]
    rows_grad = rows_all[:, width:]
    g = jnp.dot(rows_in, w_gate, preferred_element_type=jnp.float32)
    u = jnp.dot(rows_in, w_up, preferred_element_type=jnp.float32)
    dh = lax.dot_general(
        rows_grad, w_down, (((1,), (1,)), ((), ())), preferred_element_type=jnp.float32
    )
    sig = jax.nn.sigmoid(g)
    grad_gate = (dh * u * sig * (1.0 + g * (1.0 - sig))).astype(jnp.bfloat16)
    grad_up = (dh * g * sig).astype(jnp.bfloat16)
    part = lax.dot_general(
        grad_gate, w_gate, (((1,), (1,)), ((), ())), preferred_element_type=jnp.float32
    )
    part = part + lax.dot_general(
        grad_up, w_up, (((1,), (1,)), ((), ())), preferred_element_type=jnp.float32
    )
    return part.astype(jnp.bfloat16)


def dispatch(slots):
    count = lax.axis_size("z")
    pieces = []
    for d in range(count):
        if d == 0:
            received = slots[0]
        else:
            received = lax.ppermute(slots[d], "z", [(i, i ^ d) for i in range(count)])
        across = jnp.stack([received, swap(received, "x")])
        pieces.append(jnp.stack([across, swap(across, "c")]))
    return jnp.stack(pieces, axis=2)


def reduce_group(partial):
    from_core = swap(partial[1], "c")
    chip_sum = partial[0].astype(jnp.float32) + from_core.astype(jnp.float32)
    totals = []
    for d in range(chip_sum.shape[1]):
        from_x = swap(chip_sum[1, d].astype(jnp.bfloat16), "x")
        totals.append((chip_sum[0, d] + from_x.astype(jnp.float32)).astype(jnp.bfloat16))
    return totals


def returned(totals):
    count = lax.axis_size("z")
    out = [totals[0]]
    for d in range(1, count):
        out.append(lax.ppermute(totals[d], "z", [(i, i ^ d) for i in range(count)]))
    return jnp.stack(out)


def body(
    fwd_input,
    fwd_experts,
    fwd_gates,
    bwd_input,
    bwd_grad,
    bwd_experts,
    bwd_gates,
    gate_proj,
    up_proj,
    down_proj,
):
    experts = lax.axis_size("z")
    tokens = fwd_input.shape[1]
    width = fwd_input.shape[2]
    capacity = min(tokens, 3 * tokens * TOPK // (2 * experts))
    w_gate = gate_proj[0]
    w_up = up_proj[0]
    w_down = down_proj[0]
    here = lax.axis_index("z")
    f_select, f_weights = routing(fwd_experts[0] ^ here, fwd_gates[0], experts, capacity)
    b_select, b_weights = routing(bwd_experts[0] ^ here, bwd_gates[0], experts, capacity)
    f_slots = into_slots(f_select, fwd_input[0]).reshape(experts, capacity, width)
    b_joined = jnp.concatenate([bwd_input[0], bwd_grad[0]], axis=1)
    b_slots = into_slots(b_select, b_joined).reshape(experts, capacity, 2 * width)
    f_rows = dispatch(f_slots)
    b_rows = dispatch(b_slots)
    f_partial = forward_rows(f_rows.reshape(-1, width), w_gate, w_up, w_down)
    f_totals = reduce_group(f_partial.reshape(2, 2, experts, capacity, width))
    b_rows, f_totals = lax.optimization_barrier((b_rows, f_totals))
    f_out = returned(f_totals)
    b_partial = backward_rows(b_rows.reshape(-1, 2 * width), w_gate, w_up, w_down)
    b_partial, f_out = lax.optimization_barrier((b_partial, f_out))
    b_out = returned(reduce_group(b_partial.reshape(2, 2, experts, capacity, width)))
    high = lax.Precision.HIGHEST
    f_mixed = jnp.dot(
        f_weights, f_out.reshape(experts * capacity, width).astype(jnp.float32), precision=high
    )
    f_result = (fwd_input[0].astype(jnp.float32) + f_mixed).astype(jnp.bfloat16)
    b_mixed = jnp.dot(
        b_weights, b_out.reshape(experts * capacity, width).astype(jnp.float32), precision=high
    )
    b_result = (bwd_grad[0].astype(jnp.float32) + b_mixed).astype(jnp.bfloat16)
    next_section_input = passed_along(f_result[None], "pp", 1)
    prev_section_grad = passed_along(b_result[None], "pp", -1)
    return (next_section_input, prev_section_grad)


def solution(mesh):
    sections = mesh.shape["pp"]
    devices = mesh.shape["ep"]
    grid = mesh.devices.reshape(sections, devices // GROUP, 2, 2)
    split = Mesh(grid, ("pp",) + EP)
    rows = P("pp", EP, None)
    columns = P("pp", None, EP)
    in_specs = (rows, rows, rows, rows, rows, rows, rows, columns, columns, rows)
    out_specs = (rows, rows)
    return jax.shard_map(body, mesh=split, in_specs=in_specs, out_specs=out_specs, check_vma=False)
```

```python
import jax
import jax.numpy as jnp
from jax import lax
from jax.sharding import Mesh
from jax.sharding import PartitionSpec as P

GROUP = 4
TOPK = 2
EP = ("z", "x", "c")


def swap(value, axis):
    return lax.ppermute(value, axis, [(0, 1), (1, 0)])


def passed_along(value, axis, steps):
    count = lax.axis_size(axis)
    pairs = [(source, (source + steps) % count) for source in range(count)]
    return lax.ppermute(value, axis, pairs)


def routing(ids, gates, experts, capacity):
    pairs = ids.reshape(-1)
    hot = (pairs[:, None] == jnp.arange(experts, dtype=jnp.int32)[None, :]).astype(jnp.int32)
    before = jnp.cumsum(hot, axis=0) - hot
    slot = jnp.sum(hot * before, axis=1)
    target = (pairs * capacity + slot).reshape(ids.shape)
    columns = jnp.arange(experts * capacity, dtype=jnp.int32)
    match = (target[:, :, None] == columns[None, None, :]).astype(jnp.float32)
    select = jnp.sum(match, axis=1).astype(jnp.bfloat16)
    weights = jnp.sum(gates[:, :, None] * match, axis=1)
    return (select, weights)


def into_slots(select, rows_in):
    placed = lax.dot_general(
        select, rows_in, (((0,), (0,)), ((), ())), preferred_element_type=jnp.float32
    )
    return placed.astype(jnp.bfloat16)


def forward_rows(rows_in, w_gate, w_up, w_down):
    g = jnp.dot(rows_in, w_gate, preferred_element_type=jnp.float32)
    u = jnp.dot(rows_in, w_up, preferred_element_type=jnp.float32)
    hidden = (g * jax.nn.sigmoid(g) * u).astype(jnp.bfloat16)
    return jnp.dot(hidden, w_down, preferred_element_type=jnp.float32).astype(jnp.bfloat16)


def backward_rows(rows_all, w_gate, w_up, w_down):
    width = w_gate.shape[0]
    rows_in = rows_all[:, :width]
    rows_grad = rows_all[:, width:]
    g = jnp.dot(rows_in, w_gate, preferred_element_type=jnp.float32)
    u = jnp.dot(rows_in, w_up, preferred_element_type=jnp.float32)
    dh = lax.dot_general(
        rows_grad, w_down, (((1,), (1,)), ((), ())), preferred_element_type=jnp.float32
    )
    sig = jax.nn.sigmoid(g)
    grad_gate = (dh * u * sig * (1.0 + g * (1.0 - sig))).astype(jnp.bfloat16)
    grad_up = (dh * g * sig).astype(jnp.bfloat16)
    part = lax.dot_general(
        grad_gate, w_gate, (((1,), (1,)), ((), ())), preferred_element_type=jnp.float32
    )
    part = part + lax.dot_general(
        grad_up, w_up, (((1,), (1,)), ((), ())), preferred_element_type=jnp.float32
    )
    return part.astype(jnp.bfloat16)


def dispatch(slots):
    count = lax.axis_size("z")
    pieces = []
    for d in range(count):
        if d == 0:
            received = slots[0]
        else:
            received = lax.ppermute(slots[d], "z", [(i, i ^ d) for i in range(count)])
        across = jnp.stack([received, swap(received, "x")])
        pieces.append(jnp.stack([across, swap(across, "c")]))
    return jnp.stack(pieces, axis=2)


def reduce_group(partial):
    from_core = swap(partial[1], "c")
    chip_sum = partial[0].astype(jnp.float32) + from_core.astype(jnp.float32)
    totals = []
    for d in range(chip_sum.shape[1]):
        from_x = swap(chip_sum[1, d].astype(jnp.bfloat16), "x")
        totals.append((chip_sum[0, d] + from_x.astype(jnp.float32)).astype(jnp.bfloat16))
    return totals


def returned(totals):
    count = lax.axis_size("z")
    out = [totals[0]]
    for d in range(1, count):
        out.append(lax.ppermute(totals[d], "z", [(i, i ^ d) for i in range(count)]))
    return jnp.stack(out)


def body(
    fwd_input,
    fwd_experts,
    fwd_gates,
    bwd_input,
    bwd_grad,
    bwd_experts,
    bwd_gates,
    gate_proj,
    up_proj,
    down_proj,
):
    experts = lax.axis_size("z")
    tokens = fwd_input.shape[1]
    width = fwd_input.shape[2]
    capacity = min(tokens, 3 * tokens * TOPK // (2 * experts))
    w_gate = gate_proj[0]
    w_up = up_proj[0]
    w_down = down_proj[0]
    here = lax.axis_index("z")
    f_select, f_weights = routing(fwd_experts[0] ^ here, fwd_gates[0], experts, capacity)
    b_select, b_weights = routing(bwd_experts[0] ^ here, bwd_gates[0], experts, capacity)
    f_slots = into_slots(f_select, fwd_input[0]).reshape(experts, capacity, width)
    b_joined = jnp.concatenate([bwd_input[0], bwd_grad[0]], axis=1)
    b_slots = into_slots(b_select, b_joined).reshape(experts, capacity, 2 * width)
    b_rows = dispatch(b_slots)
    f_rows = dispatch(f_slots)
    b_partial = backward_rows(b_rows.reshape(-1, 2 * width), w_gate, w_up, w_down)
    b_totals = reduce_group(b_partial.reshape(2, 2, experts, capacity, width))
    f_rows, b_totals = lax.optimization_barrier((f_rows, b_totals))
    b_out = returned(b_totals)
    f_partial = forward_rows(f_rows.reshape(-1, width), w_gate, w_up, w_down)
    f_out = returned(reduce_group(f_partial.reshape(2, 2, experts, capacity, width)))
    high = lax.Precision.HIGHEST
    f_mixed = jnp.dot(
        f_weights, f_out.reshape(experts * capacity, width).astype(jnp.float32), precision=high
    )
    f_result = (fwd_input[0].astype(jnp.float32) + f_mixed).astype(jnp.bfloat16)
    b_mixed = jnp.dot(
        b_weights, b_out.reshape(experts * capacity, width).astype(jnp.float32), precision=high
    )
    b_result = (bwd_grad[0].astype(jnp.float32) + b_mixed).astype(jnp.bfloat16)
    next_section_input = passed_along(f_result[None], "pp", 1)
    prev_section_grad = passed_along(b_result[None], "pp", -1)
    return (next_section_input, prev_section_grad)


def solution(mesh):
    sections = mesh.shape["pp"]
    devices = mesh.shape["ep"]
    grid = mesh.devices.reshape(sections, devices // GROUP, 2, 2)
    split = Mesh(grid, ("pp",) + EP)
    rows = P("pp", EP, None)
    columns = P("pp", None, EP)
    in_specs = (rows, rows, rows, rows, rows, rows, rows, columns, columns, rows)
    out_specs = (rows, rows)
    return jax.shard_map(body, mesh=split, in_specs=in_specs, out_specs=out_specs, check_vma=False)
```

```python
import jax
import jax.numpy as jnp
from jax import lax
from jax.sharding import Mesh
from jax.sharding import PartitionSpec as P

GROUP = 4
TOPK = 2
EP = ("z", "x", "c")


def swap(value, axis):
    return lax.ppermute(value, axis, [(0, 1), (1, 0)])


def passed_along(value, axis, steps):
    count = lax.axis_size(axis)
    pairs = [(source, (source + steps) % count) for source in range(count)]
    return lax.ppermute(value, axis, pairs)


def routing(ids, gates, experts, capacity):
    pairs = ids.reshape(-1)
    hot = (pairs[:, None] == jnp.arange(experts, dtype=jnp.int32)[None, :]).astype(jnp.int32)
    before = jnp.cumsum(hot, axis=0) - hot
    slot = jnp.sum(hot * before, axis=1)
    target = (pairs * capacity + slot).reshape(ids.shape)
    columns = jnp.arange(experts * capacity, dtype=jnp.int32)
    match = (target[:, :, None] == columns[None, None, :]).astype(jnp.float32)
    select = jnp.sum(match, axis=1).astype(jnp.bfloat16)
    weights = jnp.sum(gates[:, :, None] * match, axis=1)
    return (select, weights)


def into_slots(select, rows_in):
    placed = lax.dot_general(
        select, rows_in, (((0,), (0,)), ((), ())), preferred_element_type=jnp.float32
    )
    return placed.astype(jnp.bfloat16)


def forward_rows(rows_in, w_gate, w_up, w_down):
    g = jnp.dot(rows_in, w_gate, preferred_element_type=jnp.float32)
    u = jnp.dot(rows_in, w_up, preferred_element_type=jnp.float32)
    hidden = (g * jax.nn.sigmoid(g) * u).astype(jnp.bfloat16)
    return jnp.dot(hidden, w_down, preferred_element_type=jnp.float32).astype(jnp.bfloat16)


def backward_rows(rows_all, w_gate, w_up, w_down):
    width = w_gate.shape[0]
    rows_in = rows_all[:, :width]
    rows_grad = rows_all[:, width:]
    g = jnp.dot(rows_in, w_gate, preferred_element_type=jnp.float32)
    u = jnp.dot(rows_in, w_up, preferred_element_type=jnp.float32)
    dh = lax.dot_general(
        rows_grad, w_down, (((1,), (1,)), ((), ())), preferred_element_type=jnp.float32
    )
    sig = jax.nn.sigmoid(g)
    grad_gate = (dh * u * sig * (1.0 + g * (1.0 - sig))).astype(jnp.bfloat16)
    grad_up = (dh * g * sig).astype(jnp.bfloat16)
    part = lax.dot_general(
        grad_gate, w_gate, (((1,), (1,)), ((), ())), preferred_element_type=jnp.float32
    )
    part = part + lax.dot_general(
        grad_up, w_up, (((1,), (1,)), ((), ())), preferred_element_type=jnp.float32
    )
    return part.astype(jnp.bfloat16)


def dispatch(slots):
    count = lax.axis_size("z")
    pieces = []
    for d in range(count):
        if d == 0:
            received = slots[0]
        else:
            received = lax.ppermute(slots[d], "z", [(i, i ^ d) for i in range(count)])
        across = jnp.stack([received, swap(received, "x")])
        pieces.append(jnp.stack([across, swap(across, "c")]))
    return jnp.stack(pieces, axis=2)


def reduce_group(partial):
    from_core = swap(partial[1], "c")
    chip_sum = partial[0].astype(jnp.float32) + from_core.astype(jnp.float32)
    totals = []
    for d in range(chip_sum.shape[1]):
        from_x = swap(chip_sum[1, d].astype(jnp.bfloat16), "x")
        totals.append((chip_sum[0, d] + from_x.astype(jnp.float32)).astype(jnp.bfloat16))
    return totals


def returned(totals):
    count = lax.axis_size("z")
    out = [totals[0]]
    for d in range(1, count):
        out.append(lax.ppermute(totals[d], "z", [(i, i ^ d) for i in range(count)]))
    return jnp.stack(out)


def body(
    fwd_input,
    fwd_experts,
    fwd_gates,
    bwd_input,
    bwd_grad,
    bwd_experts,
    bwd_gates,
    gate_proj,
    up_proj,
    down_proj,
):
    experts = lax.axis_size("z")
    tokens = fwd_input.shape[1]
    width = fwd_input.shape[2]
    capacity = min(tokens, 3 * tokens * TOPK // (2 * experts))
    w_gate = gate_proj[0]
    w_up = up_proj[0]
    w_down = down_proj[0]
    here = lax.axis_index("z")
    f_select, f_weights = routing(fwd_experts[0] ^ here, fwd_gates[0], experts, capacity)
    b_select, b_weights = routing(bwd_experts[0] ^ here, bwd_gates[0], experts, capacity)
    joined = jnp.concatenate([fwd_input[0], bwd_input[0], bwd_grad[0]], axis=1)
    f_slots = into_slots(f_select, fwd_input[0])
    b_slots = into_slots(b_select, joined[:, width:])
    both = jnp.concatenate([f_slots, b_slots], axis=1).reshape(experts, capacity, 3 * width)
    rows = dispatch(both).reshape(-1, 3 * width)
    f_rows = rows[:, :width]
    b_rows = rows[:, width:]
    f_partial = forward_rows(f_rows, w_gate, w_up, w_down)
    f_totals = reduce_group(f_partial.reshape(2, 2, experts, capacity, width))
    b_rows, f_totals = lax.optimization_barrier((b_rows, f_totals))
    f_out = returned(f_totals)
    b_partial = backward_rows(b_rows, w_gate, w_up, w_down)
    b_out = returned(reduce_group(b_partial.reshape(2, 2, experts, capacity, width)))
    high = lax.Precision.HIGHEST
    f_mixed = jnp.dot(
        f_weights, f_out.reshape(experts * capacity, width).astype(jnp.float32), precision=high
    )
    f_result = (fwd_input[0].astype(jnp.float32) + f_mixed).astype(jnp.bfloat16)
    b_mixed = jnp.dot(
        b_weights, b_out.reshape(experts * capacity, width).astype(jnp.float32), precision=high
    )
    b_result = (bwd_grad[0].astype(jnp.float32) + b_mixed).astype(jnp.bfloat16)
    next_section_input = passed_along(f_result[None], "pp", 1)
    prev_section_grad = passed_along(b_result[None], "pp", -1)
    return (next_section_input, prev_section_grad)


def solution(mesh):
    sections = mesh.shape["pp"]
    devices = mesh.shape["ep"]
    grid = mesh.devices.reshape(sections, devices // GROUP, 2, 2)
    split = Mesh(grid, ("pp",) + EP)
    rows = P("pp", EP, None)
    columns = P("pp", None, EP)
    in_specs = (rows, rows, rows, rows, rows, rows, rows, columns, columns, rows)
    out_specs = (rows, rows)
    return jax.shard_map(body, mesh=split, in_specs=in_specs, out_specs=out_specs, check_vma=False)
```

```python
import jax
import jax.numpy as jnp
from jax import lax
from jax.sharding import Mesh
from jax.sharding import PartitionSpec as P

GROUP = 4
TOPK = 2
EP = ("z", "x", "c")


def swap(value, axis):
    return lax.ppermute(value, axis, [(0, 1), (1, 0)])


def passed_along(value, axis, steps):
    count = lax.axis_size(axis)
    pairs = [(source, (source + steps) % count) for source in range(count)]
    return lax.ppermute(value, axis, pairs)


def routing(ids, gates, experts, capacity):
    pairs = ids.reshape(-1)
    hot = (pairs[:, None] == jnp.arange(experts, dtype=jnp.int32)[None, :]).astype(jnp.int32)
    before = jnp.cumsum(hot, axis=0) - hot
    slot = jnp.sum(hot * before, axis=1)
    target = (pairs * capacity + slot).reshape(ids.shape)
    columns = jnp.arange(experts * capacity, dtype=jnp.int32)
    match = (target[:, :, None] == columns[None, None, :]).astype(jnp.float32)
    select = jnp.sum(match, axis=1).astype(jnp.bfloat16)
    weights = jnp.sum(gates[:, :, None] * match, axis=1)
    return (select, weights)


def into_slots(select, rows_in):
    placed = lax.dot_general(
        select, rows_in, (((0,), (0,)), ((), ())), preferred_element_type=jnp.float32
    )
    return placed.astype(jnp.bfloat16)


def forward_rows(rows_in, w_gate, w_up, w_down):
    g = jnp.dot(rows_in, w_gate, preferred_element_type=jnp.float32)
    u = jnp.dot(rows_in, w_up, preferred_element_type=jnp.float32)
    hidden = (g * jax.nn.sigmoid(g) * u).astype(jnp.bfloat16)
    return jnp.dot(hidden, w_down, preferred_element_type=jnp.float32).astype(jnp.bfloat16)


def backward_rows(rows_all, w_gate, w_up, w_down):
    width = w_gate.shape[0]
    rows_in = rows_all[:, :width]
    rows_grad = rows_all[:, width:]
    g = jnp.dot(rows_in, w_gate, preferred_element_type=jnp.float32)
    u = jnp.dot(rows_in, w_up, preferred_element_type=jnp.float32)
    dh = lax.dot_general(
        rows_grad, w_down, (((1,), (1,)), ((), ())), preferred_element_type=jnp.float32
    )
    sig = jax.nn.sigmoid(g)
    grad_gate = (dh * u * sig * (1.0 + g * (1.0 - sig))).astype(jnp.bfloat16)
    grad_up = (dh * g * sig).astype(jnp.bfloat16)
    part = lax.dot_general(
        grad_gate, w_gate, (((1,), (1,)), ((), ())), preferred_element_type=jnp.float32
    )
    part = part + lax.dot_general(
        grad_up, w_up, (((1,), (1,)), ((), ())), preferred_element_type=jnp.float32
    )
    return part.astype(jnp.bfloat16)


def dispatch(slots):
    count = lax.axis_size("z")
    pieces = []
    for d in range(count):
        if d == 0:
            received = slots[0]
        else:
            received = lax.ppermute(slots[d], "z", [(i, i ^ d) for i in range(count)])
        across = jnp.stack([received, swap(received, "x")])
        pieces.append(jnp.stack([across, swap(across, "c")]))
    return jnp.stack(pieces, axis=2)


def chip_reduce(partial):
    from_core = swap(partial[1], "c")
    return partial[0].astype(jnp.float32) + from_core.astype(jnp.float32)


def x_reduce(chip_sum):
    totals = []
    for d in range(chip_sum.shape[1]):
        from_x = swap(chip_sum[1, d].astype(jnp.bfloat16), "x")
        totals.append((chip_sum[0, d] + from_x.astype(jnp.float32)).astype(jnp.bfloat16))
    return totals


def returned(totals):
    count = lax.axis_size("z")
    out = [totals[0]]
    for d in range(1, count):
        out.append(lax.ppermute(totals[d], "z", [(i, i ^ d) for i in range(count)]))
    return jnp.stack(out)


def body(
    fwd_input,
    fwd_experts,
    fwd_gates,
    bwd_input,
    bwd_grad,
    bwd_experts,
    bwd_gates,
    gate_proj,
    up_proj,
    down_proj,
):
    experts = lax.axis_size("z")
    tokens = fwd_input.shape[1]
    width = fwd_input.shape[2]
    capacity = min(tokens, 3 * tokens * TOPK // (2 * experts))
    w_gate = gate_proj[0]
    w_up = up_proj[0]
    w_down = down_proj[0]
    here = lax.axis_index("z")
    f_select, f_weights = routing(fwd_experts[0] ^ here, fwd_gates[0], experts, capacity)
    b_select, b_weights = routing(bwd_experts[0] ^ here, bwd_gates[0], experts, capacity)
    f_slots = into_slots(f_select, fwd_input[0]).reshape(experts, capacity, width)
    b_joined = jnp.concatenate([bwd_input[0], bwd_grad[0]], axis=1)
    b_slots = into_slots(b_select, b_joined).reshape(experts, capacity, 2 * width)
    f_rows = dispatch(f_slots)
    b_rows = dispatch(b_slots)
    f_partial = forward_rows(f_rows.reshape(-1, width), w_gate, w_up, w_down)
    f_chip = chip_reduce(f_partial.reshape(2, 2, experts, capacity, width))
    b_rows, f_chip = lax.optimization_barrier((b_rows, f_chip))
    f_out = returned(x_reduce(f_chip))
    b_partial = backward_rows(b_rows.reshape(-1, 2 * width), w_gate, w_up, w_down)
    b_out = returned(x_reduce(chip_reduce(b_partial.reshape(2, 2, experts, capacity, width))))
    high = lax.Precision.HIGHEST
    f_mixed = jnp.dot(
        f_weights, f_out.reshape(experts * capacity, width).astype(jnp.float32), precision=high
    )
    f_result = (fwd_input[0].astype(jnp.float32) + f_mixed).astype(jnp.bfloat16)
    b_mixed = jnp.dot(
        b_weights, b_out.reshape(experts * capacity, width).astype(jnp.float32), precision=high
    )
    b_result = (bwd_grad[0].astype(jnp.float32) + b_mixed).astype(jnp.bfloat16)
    next_section_input = passed_along(f_result[None], "pp", 1)
    prev_section_grad = passed_along(b_result[None], "pp", -1)
    return (next_section_input, prev_section_grad)


def solution(mesh):
    sections = mesh.shape["pp"]
    devices = mesh.shape["ep"]
    grid = mesh.devices.reshape(sections, devices // GROUP, 2, 2)
    split = Mesh(grid, ("pp",) + EP)
    rows = P("pp", EP, None)
    columns = P("pp", None, EP)
    in_specs = (rows, rows, rows, rows, rows, rows, rows, columns, columns, rows)
    out_specs = (rows, rows)
    return jax.shard_map(body, mesh=split, in_specs=in_specs, out_specs=out_specs, check_vma=False)
```

```python
import jax
import jax.numpy as jnp
from jax import lax
from jax.sharding import Mesh
from jax.sharding import PartitionSpec as P

GROUP = 4
TOPK = 2
EP = ("z", "x", "c")


def swap(value, axis):
    return lax.ppermute(value, axis, [(0, 1), (1, 0)])


def passed_along(value, axis, steps):
    count = lax.axis_size(axis)
    pairs = [(source, (source + steps) % count) for source in range(count)]
    return lax.ppermute(value, axis, pairs)


def routing(ids, gates, experts, capacity):
    pairs = ids.reshape(-1)
    hot = (pairs[:, None] == jnp.arange(experts, dtype=jnp.int32)[None, :]).astype(jnp.int32)
    before = jnp.cumsum(hot, axis=0) - hot
    slot = jnp.sum(hot * before, axis=1)
    target = (pairs * capacity + slot).reshape(ids.shape)
    columns = jnp.arange(experts * capacity, dtype=jnp.int32)
    match = (target[:, :, None] == columns[None, None, :]).astype(jnp.float32)
    select = jnp.sum(match, axis=1).astype(jnp.bfloat16)
    weights = jnp.sum(gates[:, :, None] * match, axis=1)
    return (select, weights)


def into_slots(select, rows_in):
    placed = lax.dot_general(
        select, rows_in, (((0,), (0,)), ((), ())), preferred_element_type=jnp.float32
    )
    return placed.astype(jnp.bfloat16)


def forward_rows(rows_in, w_gate, w_up, w_down):
    g = jnp.dot(rows_in, w_gate, preferred_element_type=jnp.float32)
    u = jnp.dot(rows_in, w_up, preferred_element_type=jnp.float32)
    hidden = (g * jax.nn.sigmoid(g) * u).astype(jnp.bfloat16)
    return jnp.dot(hidden, w_down, preferred_element_type=jnp.float32).astype(jnp.bfloat16)


def backward_rows(rows_all, w_gate, w_up, w_down):
    width = w_gate.shape[0]
    rows_in = rows_all[:, :width]
    rows_grad = rows_all[:, width:]
    g = jnp.dot(rows_in, w_gate, preferred_element_type=jnp.float32)
    u = jnp.dot(rows_in, w_up, preferred_element_type=jnp.float32)
    dh = lax.dot_general(
        rows_grad, w_down, (((1,), (1,)), ((), ())), preferred_element_type=jnp.float32
    )
    sig = jax.nn.sigmoid(g)
    grad_gate = (dh * u * sig * (1.0 + g * (1.0 - sig))).astype(jnp.bfloat16)
    grad_up = (dh * g * sig).astype(jnp.bfloat16)
    part = lax.dot_general(
        grad_gate, w_gate, (((1,), (1,)), ((), ())), preferred_element_type=jnp.float32
    )
    part = part + lax.dot_general(
        grad_up, w_up, (((1,), (1,)), ((), ())), preferred_element_type=jnp.float32
    )
    return part.astype(jnp.bfloat16)


def dispatch(slots):
    count = lax.axis_size("z")
    pieces = []
    for d in range(count):
        if d == 0:
            received = slots[0]
        else:
            received = lax.ppermute(slots[d], "z", [(i, i ^ d) for i in range(count)])
        across = jnp.stack([received, swap(received, "x")])
        pieces.append(jnp.stack([across, swap(across, "c")]))
    return jnp.stack(pieces, axis=2)


def reduce_group(partial):
    from_core = swap(partial[1], "c")
    chip_sum = partial[0].astype(jnp.float32) + from_core.astype(jnp.float32)
    totals = []
    for d in range(chip_sum.shape[1]):
        from_x = swap(chip_sum[1, d].astype(jnp.bfloat16), "x")
        totals.append((chip_sum[0, d] + from_x.astype(jnp.float32)).astype(jnp.bfloat16))
    return totals


def returned(totals):
    count = lax.axis_size("z")
    out = [totals[0]]
    for d in range(1, count):
        out.append(lax.ppermute(totals[d], "z", [(i, i ^ d) for i in range(count)]))
    return jnp.stack(out)


def body(
    fwd_input,
    fwd_experts,
    fwd_gates,
    bwd_input,
    bwd_grad,
    bwd_experts,
    bwd_gates,
    gate_proj,
    up_proj,
    down_proj,
):
    experts = lax.axis_size("z")
    tokens = fwd_input.shape[1]
    width = fwd_input.shape[2]
    capacity = min(tokens, 3 * tokens * TOPK // (2 * experts))
    w_gate = gate_proj[0]
    w_up = up_proj[0]
    w_down = down_proj[0]
    here = lax.axis_index("z")
    f_select, f_weights = routing(fwd_experts[0] ^ here, fwd_gates[0], experts, capacity)
    b_select, b_weights = routing(bwd_experts[0] ^ here, bwd_gates[0], experts, capacity)
    f_slots = into_slots(f_select, fwd_input[0]).reshape(experts, capacity, width)
    b_joined = jnp.concatenate([bwd_input[0], bwd_grad[0]], axis=1)
    b_slots = into_slots(b_select, b_joined).reshape(experts, capacity, 2 * width)
    f_rows = dispatch(f_slots)
    b_slots, f_rows = lax.optimization_barrier((b_slots, f_rows))
    b_rows = dispatch(b_slots)
    f_partial = forward_rows(f_rows.reshape(-1, width), w_gate, w_up, w_down)
    f_totals = reduce_group(f_partial.reshape(2, 2, experts, capacity, width))
    b_rows, f_totals = lax.optimization_barrier((b_rows, f_totals))
    f_out = returned(f_totals)
    b_partial = backward_rows(b_rows.reshape(-1, 2 * width), w_gate, w_up, w_down)
    b_out = returned(reduce_group(b_partial.reshape(2, 2, experts, capacity, width)))
    high = lax.Precision.HIGHEST
    f_mixed = jnp.dot(
        f_weights, f_out.reshape(experts * capacity, width).astype(jnp.float32), precision=high
    )
    f_result = (fwd_input[0].astype(jnp.float32) + f_mixed).astype(jnp.bfloat16)
    b_mixed = jnp.dot(
        b_weights, b_out.reshape(experts * capacity, width).astype(jnp.float32), precision=high
    )
    b_result = (bwd_grad[0].astype(jnp.float32) + b_mixed).astype(jnp.bfloat16)
    next_section_input = passed_along(f_result[None], "pp", 1)
    prev_section_grad = passed_along(b_result[None], "pp", -1)
    return (next_section_input, prev_section_grad)


def solution(mesh):
    sections = mesh.shape["pp"]
    devices = mesh.shape["ep"]
    grid = mesh.devices.reshape(sections, devices // GROUP, 2, 2)
    split = Mesh(grid, ("pp",) + EP)
    rows = P("pp", EP, None)
    columns = P("pp", None, EP)
    in_specs = (rows, rows, rows, rows, rows, rows, rows, columns, columns, rows)
    out_specs = (rows, rows)
    return jax.shard_map(body, mesh=split, in_specs=in_specs, out_specs=out_specs, check_vma=False)
```

```python
import jax
import jax.numpy as jnp
from jax import lax
from jax.sharding import Mesh
from jax.sharding import PartitionSpec as P

GROUP = 4
TOPK = 2
EP = ("z", "x", "c")


def swap(value, axis):
    return lax.ppermute(value, axis, [(0, 1), (1, 0)])


def passed_along(value, axis, steps):
    count = lax.axis_size(axis)
    pairs = [(source, (source + steps) % count) for source in range(count)]
    return lax.ppermute(value, axis, pairs)


def routing(ids, gates, experts, capacity):
    pairs = ids.reshape(-1)
    hot = (pairs[:, None] == jnp.arange(experts, dtype=jnp.int32)[None, :]).astype(jnp.int32)
    before = jnp.cumsum(hot, axis=0) - hot
    slot = jnp.sum(hot * before, axis=1)
    target = (pairs * capacity + slot).reshape(ids.shape)
    columns = jnp.arange(experts * capacity, dtype=jnp.int32)
    match = (target[:, :, None] == columns[None, None, :]).astype(jnp.float32)
    select = jnp.sum(match, axis=1).astype(jnp.bfloat16)
    weights = jnp.sum(gates[:, :, None] * match, axis=1)
    return (select, weights)


def into_slots(select, rows_in):
    placed = lax.dot_general(
        select, rows_in, (((0,), (0,)), ((), ())), preferred_element_type=jnp.float32
    )
    return placed.astype(jnp.bfloat16)


def forward_rows(rows_in, w_gate, w_up, w_down):
    g = jnp.dot(rows_in, w_gate, preferred_element_type=jnp.float32)
    u = jnp.dot(rows_in, w_up, preferred_element_type=jnp.float32)
    hidden = (g * jax.nn.sigmoid(g) * u).astype(jnp.bfloat16)
    return jnp.dot(hidden, w_down, preferred_element_type=jnp.float32).astype(jnp.bfloat16)


def backward_rows(rows_all, w_gate, w_up, w_down):
    width = w_gate.shape[0]
    rows_in = rows_all[:, :width]
    rows_grad = rows_all[:, width:]
    g = jnp.dot(rows_in, w_gate, preferred_element_type=jnp.float32)
    u = jnp.dot(rows_in, w_up, preferred_element_type=jnp.float32)
    dh = lax.dot_general(
        rows_grad, w_down, (((1,), (1,)), ((), ())), preferred_element_type=jnp.float32
    )
    sig = jax.nn.sigmoid(g)
    grad_gate = (dh * u * sig * (1.0 + g * (1.0 - sig))).astype(jnp.bfloat16)
    grad_up = (dh * g * sig).astype(jnp.bfloat16)
    part = lax.dot_general(
        grad_gate, w_gate, (((1,), (1,)), ((), ())), preferred_element_type=jnp.float32
    )
    part = part + lax.dot_general(
        grad_up, w_up, (((1,), (1,)), ((), ())), preferred_element_type=jnp.float32
    )
    return part.astype(jnp.bfloat16)


def dispatch(slots):
    count = lax.axis_size("z")
    pieces = []
    for d in range(count):
        if d == 0:
            received = slots[0]
        else:
            received = lax.ppermute(slots[d], "z", [(i, i ^ d) for i in range(count)])
        across = jnp.stack([received, swap(received, "x")])
        pieces.append(jnp.stack([across, swap(across, "c")]))
    return pieces


def reduce_group(partial):
    from_core = swap(partial[1], "c")
    chip_sum = partial[0].astype(jnp.float32) + from_core.astype(jnp.float32)
    totals = []
    for d in range(chip_sum.shape[1]):
        from_x = swap(chip_sum[1, d].astype(jnp.bfloat16), "x")
        totals.append((chip_sum[0, d] + from_x.astype(jnp.float32)).astype(jnp.bfloat16))
    return totals


def returned(totals, first=0):
    count = lax.axis_size("z")
    out = []
    for d, total in enumerate(totals, start=first):
        if d == 0:
            out.append(total)
        else:
            out.append(lax.ppermute(total, "z", [(i, i ^ d) for i in range(count)]))
    return out


def body(
    fwd_input,
    fwd_experts,
    fwd_gates,
    bwd_input,
    bwd_grad,
    bwd_experts,
    bwd_gates,
    gate_proj,
    up_proj,
    down_proj,
):
    experts = lax.axis_size("z")
    tokens = fwd_input.shape[1]
    width = fwd_input.shape[2]
    capacity = min(tokens, 3 * tokens * TOPK // (2 * experts))
    w_gate = gate_proj[0]
    w_up = up_proj[0]
    w_down = down_proj[0]
    here = lax.axis_index("z")
    f_select, f_weights = routing(fwd_experts[0] ^ here, fwd_gates[0], experts, capacity)
    b_select, b_weights = routing(bwd_experts[0] ^ here, bwd_gates[0], experts, capacity)
    f_slots = into_slots(f_select, fwd_input[0]).reshape(experts, capacity, width)
    b_joined = jnp.concatenate([bwd_input[0], bwd_grad[0]], axis=1)
    b_slots = into_slots(b_select, b_joined).reshape(experts, capacity, 2 * width)
    f_rows = jnp.stack(dispatch(f_slots), axis=2)
    b_pieces = dispatch(b_slots)
    early = experts // 2
    b_first = jnp.stack(b_pieces[:early], axis=2)
    b_second = jnp.stack(b_pieces[early:], axis=2)
    f_partial = forward_rows(f_rows.reshape(-1, width), w_gate, w_up, w_down)
    f_totals = reduce_group(f_partial.reshape(2, 2, experts, capacity, width))
    b_first, f_totals = lax.optimization_barrier((b_first, f_totals))
    f_out = jnp.stack(returned(f_totals))
    b_outs = []
    for first, rows in ((0, b_first), (early, b_second)):
        b_partial = backward_rows(rows.reshape(-1, 2 * width), w_gate, w_up, w_down)
        b_partial = b_partial.reshape(2, 2, rows.shape[2], capacity, width)
        b_outs += returned(reduce_group(b_partial), first)
    b_out = jnp.stack(b_outs)
    high = lax.Precision.HIGHEST
    f_mixed = jnp.dot(
        f_weights, f_out.reshape(experts * capacity, width).astype(jnp.float32), precision=high
    )
    f_result = (fwd_input[0].astype(jnp.float32) + f_mixed).astype(jnp.bfloat16)
    b_mixed = jnp.dot(
        b_weights, b_out.reshape(experts * capacity, width).astype(jnp.float32), precision=high
    )
    b_result = (bwd_grad[0].astype(jnp.float32) + b_mixed).astype(jnp.bfloat16)
    next_section_input = passed_along(f_result[None], "pp", 1)
    prev_section_grad = passed_along(b_result[None], "pp", -1)
    return (next_section_input, prev_section_grad)


def solution(mesh):
    sections = mesh.shape["pp"]
    devices = mesh.shape["ep"]
    grid = mesh.devices.reshape(sections, devices // GROUP, 2, 2)
    split = Mesh(grid, ("pp",) + EP)
    rows = P("pp", EP, None)
    columns = P("pp", None, EP)
    in_specs = (rows, rows, rows, rows, rows, rows, rows, columns, columns, rows)
    out_specs = (rows, rows)
    return jax.shard_map(body, mesh=split, in_specs=in_specs, out_specs=out_specs, check_vma=False)
```

```python
import jax
import jax.numpy as jnp
from jax import lax
from jax.sharding import Mesh
from jax.sharding import PartitionSpec as P

GROUP = 4
TOPK = 2
EP = ("z", "x", "c")


def swap(value, axis):
    return lax.ppermute(value, axis, [(0, 1), (1, 0)])


def passed_along(value, axis, steps):
    count = lax.axis_size(axis)
    pairs = [(source, (source + steps) % count) for source in range(count)]
    return lax.ppermute(value, axis, pairs)


def routing(ids, gates, experts, capacity):
    pairs = ids.reshape(-1)
    hot = (pairs[:, None] == jnp.arange(experts, dtype=jnp.int32)[None, :]).astype(jnp.int32)
    before = jnp.cumsum(hot, axis=0) - hot
    slot = jnp.sum(hot * before, axis=1)
    target = (pairs * capacity + slot).reshape(ids.shape)
    columns = jnp.arange(experts * capacity, dtype=jnp.int32)
    match = (target[:, :, None] == columns[None, None, :]).astype(jnp.float32)
    select = jnp.sum(match, axis=1).astype(jnp.bfloat16)
    weights = jnp.sum(gates[:, :, None] * match, axis=1)
    return (select, weights)


def into_slots(select, rows_in):
    placed = lax.dot_general(
        select, rows_in, (((0,), (0,)), ((), ())), preferred_element_type=jnp.float32
    )
    return placed.astype(jnp.bfloat16)


def forward_rows(rows_in, w_gate, w_up, w_down):
    g = jnp.dot(rows_in, w_gate, preferred_element_type=jnp.float32)
    u = jnp.dot(rows_in, w_up, preferred_element_type=jnp.float32)
    hidden = (g * jax.nn.sigmoid(g) * u).astype(jnp.bfloat16)
    return jnp.dot(hidden, w_down, preferred_element_type=jnp.float32).astype(jnp.bfloat16)


def backward_rows(rows_all, w_gate, w_up, w_down):
    width = w_gate.shape[0]
    rows_in = rows_all[:, :width]
    rows_grad = rows_all[:, width:]
    g = jnp.dot(rows_in, w_gate, preferred_element_type=jnp.float32)
    u = jnp.dot(rows_in, w_up, preferred_element_type=jnp.float32)
    dh = lax.dot_general(
        rows_grad, w_down, (((1,), (1,)), ((), ())), preferred_element_type=jnp.float32
    )
    sig = jax.nn.sigmoid(g)
    grad_gate = (dh * u * sig * (1.0 + g * (1.0 - sig))).astype(jnp.bfloat16)
    grad_up = (dh * g * sig).astype(jnp.bfloat16)
    part = lax.dot_general(
        grad_gate, w_gate, (((1,), (1,)), ((), ())), preferred_element_type=jnp.float32
    )
    part = part + lax.dot_general(
        grad_up, w_up, (((1,), (1,)), ((), ())), preferred_element_type=jnp.float32
    )
    return part.astype(jnp.bfloat16)


def dispatch(slots):
    count = lax.axis_size("z")
    pieces = []
    for d in range(count):
        if d == 0:
            received = slots[0]
        else:
            received = lax.ppermute(slots[d], "z", [(i, i ^ d) for i in range(count)])
        pieces.append(jnp.stack([received, swap(received, "x")]))
    across = jnp.stack(pieces, axis=1)
    return jnp.stack([across, swap(across, "c")])


def reduce_group(partial):
    from_core = swap(partial[1], "c")
    chip_sum = partial[0].astype(jnp.float32) + from_core.astype(jnp.float32)
    totals = []
    for d in range(chip_sum.shape[1]):
        from_x = swap(chip_sum[1, d].astype(jnp.bfloat16), "x")
        totals.append((chip_sum[0, d] + from_x.astype(jnp.float32)).astype(jnp.bfloat16))
    return totals


def returned(totals):
    count = lax.axis_size("z")
    out = [totals[0]]
    for d in range(1, count):
        out.append(lax.ppermute(totals[d], "z", [(i, i ^ d) for i in range(count)]))
    return jnp.stack(out)


def body(
    fwd_input,
    fwd_experts,
    fwd_gates,
    bwd_input,
    bwd_grad,
    bwd_experts,
    bwd_gates,
    gate_proj,
    up_proj,
    down_proj,
):
    experts = lax.axis_size("z")
    tokens = fwd_input.shape[1]
    width = fwd_input.shape[2]
    capacity = min(tokens, 3 * tokens * TOPK // (2 * experts))
    w_gate = gate_proj[0]
    w_up = up_proj[0]
    w_down = down_proj[0]
    here = lax.axis_index("z")
    f_select, f_weights = routing(fwd_experts[0] ^ here, fwd_gates[0], experts, capacity)
    b_select, b_weights = routing(bwd_experts[0] ^ here, bwd_gates[0], experts, capacity)
    f_slots = into_slots(f_select, fwd_input[0]).reshape(experts, capacity, width)
    b_joined = jnp.concatenate([bwd_input[0], bwd_grad[0]], axis=1)
    b_slots = into_slots(b_select, b_joined).reshape(experts, capacity, 2 * width)
    f_rows = dispatch(f_slots)
    b_rows = dispatch(b_slots)
    f_partial = forward_rows(f_rows.reshape(-1, width), w_gate, w_up, w_down)
    f_totals = reduce_group(f_partial.reshape(2, 2, experts, capacity, width))
    b_rows, f_totals = lax.optimization_barrier((b_rows, f_totals))
    f_out = returned(f_totals)
    b_partial = backward_rows(b_rows.reshape(-1, 2 * width), w_gate, w_up, w_down)
    b_out = returned(reduce_group(b_partial.reshape(2, 2, experts, capacity, width)))
    high = lax.Precision.HIGHEST
    f_mixed = jnp.dot(
        f_weights, f_out.reshape(experts * capacity, width).astype(jnp.float32), precision=high
    )
    f_result = (fwd_input[0].astype(jnp.float32) + f_mixed).astype(jnp.bfloat16)
    b_mixed = jnp.dot(
        b_weights, b_out.reshape(experts * capacity, width).astype(jnp.float32), precision=high
    )
    b_result = (bwd_grad[0].astype(jnp.float32) + b_mixed).astype(jnp.bfloat16)
    next_section_input = passed_along(f_result[None], "pp", 1)
    prev_section_grad = passed_along(b_result[None], "pp", -1)
    return (next_section_input, prev_section_grad)


def solution(mesh):
    sections = mesh.shape["pp"]
    devices = mesh.shape["ep"]
    grid = mesh.devices.reshape(sections, devices // GROUP, 2, 2)
    split = Mesh(grid, ("pp",) + EP)
    rows = P("pp", EP, None)
    columns = P("pp", None, EP)
    in_specs = (rows, rows, rows, rows, rows, rows, rows, columns, columns, rows)
    out_specs = (rows, rows)
    return jax.shard_map(body, mesh=split, in_specs=in_specs, out_specs=out_specs, check_vma=False)
```

```python
import jax
import jax.numpy as jnp
from jax import lax
from jax.sharding import Mesh
from jax.sharding import PartitionSpec as P

GROUP = 4
TOPK = 2
EP = ("z", "x", "c")


def swap(value, axis):
    return lax.ppermute(value, axis, [(0, 1), (1, 0)])


def passed_along(value, axis, steps):
    count = lax.axis_size(axis)
    pairs = [(source, (source + steps) % count) for source in range(count)]
    return lax.ppermute(value, axis, pairs)


def routing(ids, gates, experts, capacity):
    pairs = ids.reshape(-1)
    hot = (pairs[:, None] == jnp.arange(experts, dtype=jnp.int32)[None, :]).astype(jnp.int32)
    before = jnp.cumsum(hot, axis=0) - hot
    slot = jnp.sum(hot * before, axis=1)
    target = (pairs * capacity + slot).reshape(ids.shape)
    columns = jnp.arange(experts * capacity, dtype=jnp.int32)
    match = (target[:, :, None] == columns[None, None, :]).astype(jnp.float32)
    select = jnp.sum(match, axis=1).astype(jnp.bfloat16)
    weights = jnp.sum(gates[:, :, None] * match, axis=1)
    return (select, weights)


def into_slots(select, rows_in):
    placed = lax.dot_general(
        select, rows_in, (((0,), (0,)), ((), ())), preferred_element_type=jnp.float32
    )
    return placed.astype(jnp.bfloat16)


def forward_rows(rows_in, w_gate, w_up, w_down):
    g = jnp.dot(rows_in, w_gate, preferred_element_type=jnp.float32)
    u = jnp.dot(rows_in, w_up, preferred_element_type=jnp.float32)
    hidden = (g * jax.nn.sigmoid(g) * u).astype(jnp.bfloat16)
    return jnp.dot(hidden, w_down, preferred_element_type=jnp.float32).astype(jnp.bfloat16)


def backward_rows(rows_all, w_gate, w_up, w_down):
    width = w_gate.shape[0]
    rows_in = rows_all[:, :width]
    rows_grad = rows_all[:, width:]
    g = jnp.dot(rows_in, w_gate, preferred_element_type=jnp.float32)
    u = jnp.dot(rows_in, w_up, preferred_element_type=jnp.float32)
    dh = lax.dot_general(
        rows_grad, w_down, (((1,), (1,)), ((), ())), preferred_element_type=jnp.float32
    )
    sig = jax.nn.sigmoid(g)
    grad_gate = (dh * u * sig * (1.0 + g * (1.0 - sig))).astype(jnp.bfloat16)
    grad_up = (dh * g * sig).astype(jnp.bfloat16)
    part = lax.dot_general(
        grad_gate, w_gate, (((1,), (1,)), ((), ())), preferred_element_type=jnp.float32
    )
    part = part + lax.dot_general(
        grad_up, w_up, (((1,), (1,)), ((), ())), preferred_element_type=jnp.float32
    )
    return part.astype(jnp.bfloat16)


def dispatch(slots):
    count = lax.axis_size("z")
    pieces = []
    for d in range(count):
        if d == 0:
            received = slots[0]
        else:
            received = lax.ppermute(slots[d], "z", [(i, i ^ d) for i in range(count)])
        across = jnp.stack([received, swap(received, "x")])
        pieces.append(jnp.stack([across, swap(across, "c")]))
    return jnp.stack(pieces, axis=2)


def reduce_group(partial):
    from_core = swap(partial[1], "c")
    chip_sum = partial[0].astype(jnp.float32) + from_core.astype(jnp.float32)
    totals = []
    for d in range(chip_sum.shape[1]):
        from_x = swap(chip_sum[1, d].astype(jnp.bfloat16), "x")
        totals.append((chip_sum[0, d] + from_x.astype(jnp.float32)).astype(jnp.bfloat16))
    return totals


def returned(totals):
    count = lax.axis_size("z")
    out = [totals[0]]
    for d in range(1, count):
        out.append(lax.ppermute(totals[d], "z", [(i, i ^ d) for i in range(count)]))
    return jnp.stack(out)


def body(
    fwd_input,
    fwd_experts,
    fwd_gates,
    bwd_input,
    bwd_grad,
    bwd_experts,
    bwd_gates,
    gate_proj,
    up_proj,
    down_proj,
):
    experts = lax.axis_size("z")
    tokens = fwd_input.shape[1]
    width = fwd_input.shape[2]
    capacity = min(tokens, 3 * tokens * TOPK // (2 * experts))
    w_gate = gate_proj[0]
    w_up = up_proj[0]
    w_down = down_proj[0]
    here = lax.axis_index("z")
    f_select, f_weights = routing(fwd_experts[0] ^ here, fwd_gates[0], experts, capacity)
    b_select, b_weights = routing(bwd_experts[0] ^ here, bwd_gates[0], experts, capacity)
    f_slots = into_slots(f_select, fwd_input[0]).reshape(experts, capacity, width)
    b_joined = jnp.concatenate([bwd_input[0], bwd_grad[0]], axis=1)
    b_slots = into_slots(b_select, b_joined).reshape(experts, capacity, 2 * width)
    f_rows = dispatch(f_slots)
    f_partial = forward_rows(f_rows.reshape(-1, width), w_gate, w_up, w_down)
    early = experts // 2
    far = tuple(b_slots[d] for d in range(early, experts))
    far, f_partial = lax.optimization_barrier((far, f_partial))
    b_rows = dispatch([b_slots[d] for d in range(early)] + list(far))
    f_totals = reduce_group(f_partial.reshape(2, 2, experts, capacity, width))
    b_rows, f_totals = lax.optimization_barrier((b_rows, f_totals))
    f_out = returned(f_totals)
    b_partial = backward_rows(b_rows.reshape(-1, 2 * width), w_gate, w_up, w_down)
    b_out = returned(reduce_group(b_partial.reshape(2, 2, experts, capacity, width)))
    high = lax.Precision.HIGHEST
    f_mixed = jnp.dot(
        f_weights, f_out.reshape(experts * capacity, width).astype(jnp.float32), precision=high
    )
    f_result = (fwd_input[0].astype(jnp.float32) + f_mixed).astype(jnp.bfloat16)
    b_mixed = jnp.dot(
        b_weights, b_out.reshape(experts * capacity, width).astype(jnp.float32), precision=high
    )
    b_result = (bwd_grad[0].astype(jnp.float32) + b_mixed).astype(jnp.bfloat16)
    next_section_input = passed_along(f_result[None], "pp", 1)
    prev_section_grad = passed_along(b_result[None], "pp", -1)
    return (next_section_input, prev_section_grad)


def solution(mesh):
    sections = mesh.shape["pp"]
    devices = mesh.shape["ep"]
    grid = mesh.devices.reshape(sections, devices // GROUP, 2, 2)
    split = Mesh(grid, ("pp",) + EP)
    rows = P("pp", EP, None)
    columns = P("pp", None, EP)
    in_specs = (rows, rows, rows, rows, rows, rows, rows, columns, columns, rows)
    out_specs = (rows, rows)
    return jax.shard_map(body, mesh=split, in_specs=in_specs, out_specs=out_specs, check_vma=False)
```

```python
import jax
import jax.numpy as jnp
from jax import lax
from jax.sharding import Mesh
from jax.sharding import PartitionSpec as P

GROUP = 4
TOPK = 2
EP = ("z", "x", "c")


def swap(value, axis):
    return lax.ppermute(value, axis, [(0, 1), (1, 0)])


def passed_along(value, axis, steps):
    count = lax.axis_size(axis)
    pairs = [(source, (source + steps) % count) for source in range(count)]
    return lax.ppermute(value, axis, pairs)


def routing(ids, gates, experts, capacity):
    pairs = ids.reshape(-1)
    hot = (pairs[:, None] == jnp.arange(experts, dtype=jnp.int32)[None, :]).astype(jnp.int32)
    before = jnp.cumsum(hot, axis=0) - hot
    slot = jnp.sum(hot * before, axis=1)
    target = (pairs * capacity + slot).reshape(ids.shape)
    columns = jnp.arange(experts * capacity, dtype=jnp.int32)
    match = (target[:, :, None] == columns[None, None, :]).astype(jnp.float32)
    select = jnp.sum(match, axis=1).astype(jnp.bfloat16)
    weights = jnp.sum(gates[:, :, None] * match, axis=1)
    return (select, weights)


def into_slots(select, rows_in):
    placed = lax.dot_general(
        select, rows_in, (((0,), (0,)), ((), ())), preferred_element_type=jnp.float32
    )
    return placed.astype(jnp.bfloat16)


def forward_rows(rows_in, w_gate, w_up, w_down):
    g = jnp.dot(rows_in, w_gate, preferred_element_type=jnp.float32)
    u = jnp.dot(rows_in, w_up, preferred_element_type=jnp.float32)
    hidden = (g * jax.nn.sigmoid(g) * u).astype(jnp.bfloat16)
    return jnp.dot(hidden, w_down, preferred_element_type=jnp.float32).astype(jnp.bfloat16)


def backward_rows(rows_all, w_gate, w_up, w_down):
    width = w_gate.shape[0]
    rows_in = rows_all[:, :width]
    rows_grad = rows_all[:, width:]
    g = jnp.dot(rows_in, w_gate, preferred_element_type=jnp.float32)
    u = jnp.dot(rows_in, w_up, preferred_element_type=jnp.float32)
    dh = lax.dot_general(
        rows_grad, w_down, (((1,), (1,)), ((), ())), preferred_element_type=jnp.float32
    )
    sig = jax.nn.sigmoid(g)
    grad_gate = (dh * u * sig * (1.0 + g * (1.0 - sig))).astype(jnp.bfloat16)
    grad_up = (dh * g * sig).astype(jnp.bfloat16)
    part = lax.dot_general(
        grad_gate, w_gate, (((1,), (1,)), ((), ())), preferred_element_type=jnp.float32
    )
    part = part + lax.dot_general(
        grad_up, w_up, (((1,), (1,)), ((), ())), preferred_element_type=jnp.float32
    )
    return part.astype(jnp.bfloat16)


def z_round(chunk, d):
    count = lax.axis_size("z")
    if d == 0:
        return chunk
    return lax.ppermute(chunk, "z", [(i, i ^ d) for i in range(count)])


def spread(received):
    across = jnp.stack([received, swap(received, "x")])
    return jnp.stack([across, swap(across, "c")])


def reduce_group(partial):
    from_core = swap(partial[1], "c")
    chip_sum = partial[0].astype(jnp.float32) + from_core.astype(jnp.float32)
    totals = []
    for d in range(chip_sum.shape[1]):
        from_x = swap(chip_sum[1, d].astype(jnp.bfloat16), "x")
        totals.append((chip_sum[0, d] + from_x.astype(jnp.float32)).astype(jnp.bfloat16))
    return totals


def returned(totals):
    count = lax.axis_size("z")
    out = [totals[0]]
    for d in range(1, count):
        out.append(lax.ppermute(totals[d], "z", [(i, i ^ d) for i in range(count)]))
    return jnp.stack(out)


def body(
    fwd_input,
    fwd_experts,
    fwd_gates,
    bwd_input,
    bwd_grad,
    bwd_experts,
    bwd_gates,
    gate_proj,
    up_proj,
    down_proj,
):
    experts = lax.axis_size("z")
    tokens = fwd_input.shape[1]
    width = fwd_input.shape[2]
    capacity = min(tokens, 3 * tokens * TOPK // (2 * experts))
    w_gate = gate_proj[0]
    w_up = up_proj[0]
    w_down = down_proj[0]
    here = lax.axis_index("z")
    f_select, f_weights = routing(fwd_experts[0] ^ here, fwd_gates[0], experts, capacity)
    b_select, b_weights = routing(bwd_experts[0] ^ here, bwd_gates[0], experts, capacity)
    f_slots = into_slots(f_select, fwd_input[0]).reshape(experts, capacity, width)
    b_joined = jnp.concatenate([bwd_input[0], bwd_grad[0]], axis=1)
    b_slots = into_slots(b_select, b_joined).reshape(experts, capacity, 2 * width)
    early = experts // 2
    f_received = [z_round(f_slots[d], d) for d in range(experts)]
    f_rows = jnp.stack([spread(r) for r in f_received], axis=2)
    b_near = [z_round(b_slots[d], d) for d in range(early)]
    far = tuple(b_slots[d] for d in range(early, experts))
    far, _ = lax.optimization_barrier((far, tuple(f_received[early:])))
    b_far = [z_round(chunk, d) for d, chunk in enumerate(far, start=early)]
    b_rows = jnp.stack([spread(r) for r in b_near + b_far], axis=2)
    f_partial = forward_rows(f_rows.reshape(-1, width), w_gate, w_up, w_down)
    f_totals = reduce_group(f_partial.reshape(2, 2, experts, capacity, width))
    b_rows, f_totals = lax.optimization_barrier((b_rows, f_totals))
    f_out = returned(f_totals)
    b_partial = backward_rows(b_rows.reshape(-1, 2 * width), w_gate, w_up, w_down)
    b_out = returned(reduce_group(b_partial.reshape(2, 2, experts, capacity, width)))
    high = lax.Precision.HIGHEST
    f_mixed = jnp.dot(
        f_weights, f_out.reshape(experts * capacity, width).astype(jnp.float32), precision=high
    )
    f_result = (fwd_input[0].astype(jnp.float32) + f_mixed).astype(jnp.bfloat16)
    b_mixed = jnp.dot(
        b_weights, b_out.reshape(experts * capacity, width).astype(jnp.float32), precision=high
    )
    b_result = (bwd_grad[0].astype(jnp.float32) + b_mixed).astype(jnp.bfloat16)
    next_section_input = passed_along(f_result[None], "pp", 1)
    prev_section_grad = passed_along(b_result[None], "pp", -1)
    return (next_section_input, prev_section_grad)


def solution(mesh):
    sections = mesh.shape["pp"]
    devices = mesh.shape["ep"]
    grid = mesh.devices.reshape(sections, devices // GROUP, 2, 2)
    split = Mesh(grid, ("pp",) + EP)
    rows = P("pp", EP, None)
    columns = P("pp", None, EP)
    in_specs = (rows, rows, rows, rows, rows, rows, rows, columns, columns, rows)
    out_specs = (rows, rows)
    return jax.shard_map(body, mesh=split, in_specs=in_specs, out_specs=out_specs, check_vma=False)
```

```python
import jax
import jax.numpy as jnp
from jax import lax
from jax.sharding import Mesh
from jax.sharding import PartitionSpec as P

GROUP = 4
TOPK = 2
EP = ("z", "x", "c")


def swap(value, axis):
    return lax.ppermute(value, axis, [(0, 1), (1, 0)])


def passed_along(value, axis, steps):
    count = lax.axis_size(axis)
    pairs = [(source, (source + steps) % count) for source in range(count)]
    return lax.ppermute(value, axis, pairs)


def routing(ids, gates, experts, capacity):
    pairs = ids.reshape(-1)
    hot = (pairs[:, None] == jnp.arange(experts, dtype=jnp.int32)[None, :]).astype(jnp.int32)
    before = jnp.cumsum(hot, axis=0) - hot
    slot = jnp.sum(hot * before, axis=1)
    target = (pairs * capacity + slot).reshape(ids.shape)
    columns = jnp.arange(experts * capacity, dtype=jnp.int32)
    match = (target[:, :, None] == columns[None, None, :]).astype(jnp.float32)
    select = jnp.sum(match, axis=1).astype(jnp.bfloat16)
    weights = jnp.sum(gates[:, :, None] * match, axis=1)
    return (select, weights)


def into_slots(select, rows_in):
    placed = lax.dot_general(
        select, rows_in, (((0,), (0,)), ((), ())), preferred_element_type=jnp.float32
    )
    return placed.astype(jnp.bfloat16)


def forward_rows(rows_in, w_gate, w_up, w_down):
    g = jnp.dot(rows_in, w_gate, preferred_element_type=jnp.float32)
    u = jnp.dot(rows_in, w_up, preferred_element_type=jnp.float32)
    hidden = (g * jax.nn.sigmoid(g) * u).astype(jnp.bfloat16)
    return jnp.dot(hidden, w_down, preferred_element_type=jnp.float32).astype(jnp.bfloat16)


def backward_rows(rows_all, w_gate, w_up, w_down):
    width = w_gate.shape[0]
    rows_in = rows_all[:, :width]
    rows_grad = rows_all[:, width:]
    g = jnp.dot(rows_in, w_gate, preferred_element_type=jnp.float32)
    u = jnp.dot(rows_in, w_up, preferred_element_type=jnp.float32)
    dh = lax.dot_general(
        rows_grad, w_down, (((1,), (1,)), ((), ())), preferred_element_type=jnp.float32
    )
    sig = jax.nn.sigmoid(g)
    grad_gate = (dh * u * sig * (1.0 + g * (1.0 - sig))).astype(jnp.bfloat16)
    grad_up = (dh * g * sig).astype(jnp.bfloat16)
    part = lax.dot_general(
        grad_gate, w_gate, (((1,), (1,)), ((), ())), preferred_element_type=jnp.float32
    )
    part = part + lax.dot_general(
        grad_up, w_up, (((1,), (1,)), ((), ())), preferred_element_type=jnp.float32
    )
    return part.astype(jnp.bfloat16)


def z_round(chunk, d):
    count = lax.axis_size("z")
    if d == 0:
        return chunk
    return lax.ppermute(chunk, "z", [(i, i ^ d) for i in range(count)])


def spread(received):
    across = jnp.stack([received, swap(received, "x")])
    return jnp.stack([across, swap(across, "c")])


def reduce_group(partial):
    from_core = swap(partial[1], "c")
    chip_sum = partial[0].astype(jnp.float32) + from_core.astype(jnp.float32)
    totals = []
    for d in range(chip_sum.shape[1]):
        from_x = swap(chip_sum[1, d].astype(jnp.bfloat16), "x")
        totals.append((chip_sum[0, d] + from_x.astype(jnp.float32)).astype(jnp.bfloat16))
    return totals


def returned(totals):
    count = lax.axis_size("z")
    out = [totals[0]]
    for d in range(1, count):
        out.append(lax.ppermute(totals[d], "z", [(i, i ^ d) for i in range(count)]))
    return jnp.stack(out)


def body(
    fwd_input,
    fwd_experts,
    fwd_gates,
    bwd_input,
    bwd_grad,
    bwd_experts,
    bwd_gates,
    gate_proj,
    up_proj,
    down_proj,
):
    experts = lax.axis_size("z")
    tokens = fwd_input.shape[1]
    width = fwd_input.shape[2]
    capacity = min(tokens, 3 * tokens * TOPK // (2 * experts))
    w_gate = gate_proj[0]
    w_up = up_proj[0]
    w_down = down_proj[0]
    here = lax.axis_index("z")
    f_select, f_weights = routing(fwd_experts[0] ^ here, fwd_gates[0], experts, capacity)
    b_select, b_weights = routing(bwd_experts[0] ^ here, bwd_gates[0], experts, capacity)
    f_slots = into_slots(f_select, fwd_input[0]).reshape(experts, capacity, width)
    b_joined = jnp.concatenate([bwd_input[0], bwd_grad[0]], axis=1)
    b_slots = into_slots(b_select, b_joined).reshape(experts, capacity, 2 * width)
    early = experts // 2
    f_rows = jnp.stack([spread(z_round(f_slots[d], d)) for d in range(experts)], axis=2)
    b_received = [z_round(b_slots[d], d) for d in range(experts)]
    b_near = [spread(r) for r in b_received[:early]]
    f_partial = forward_rows(f_rows.reshape(-1, width), w_gate, w_up, w_down)
    f_totals = reduce_group(f_partial.reshape(2, 2, experts, capacity, width))
    b_far, f_totals = lax.optimization_barrier((tuple(b_received[early:]), f_totals))
    b_rows = jnp.stack(b_near + [spread(r) for r in b_far], axis=2)
    f_out = returned(f_totals)
    b_partial = backward_rows(b_rows.reshape(-1, 2 * width), w_gate, w_up, w_down)
    b_out = returned(reduce_group(b_partial.reshape(2, 2, experts, capacity, width)))
    high = lax.Precision.HIGHEST
    f_mixed = jnp.dot(
        f_weights, f_out.reshape(experts * capacity, width).astype(jnp.float32), precision=high
    )
    f_result = (fwd_input[0].astype(jnp.float32) + f_mixed).astype(jnp.bfloat16)
    b_mixed = jnp.dot(
        b_weights, b_out.reshape(experts * capacity, width).astype(jnp.float32), precision=high
    )
    b_result = (bwd_grad[0].astype(jnp.float32) + b_mixed).astype(jnp.bfloat16)
    next_section_input = passed_along(f_result[None], "pp", 1)
    prev_section_grad = passed_along(b_result[None], "pp", -1)
    return (next_section_input, prev_section_grad)


def solution(mesh):
    sections = mesh.shape["pp"]
    devices = mesh.shape["ep"]
    grid = mesh.devices.reshape(sections, devices // GROUP, 2, 2)
    split = Mesh(grid, ("pp",) + EP)
    rows = P("pp", EP, None)
    columns = P("pp", None, EP)
    in_specs = (rows, rows, rows, rows, rows, rows, rows, columns, columns, rows)
    out_specs = (rows, rows)
    return jax.shard_map(body, mesh=split, in_specs=in_specs, out_specs=out_specs, check_vma=False)
```

```python
import jax
import jax.numpy as jnp
from jax import lax
from jax.sharding import Mesh
from jax.sharding import PartitionSpec as P

GROUP = 4
TOPK = 2
EP = ("z", "x", "c")


def swap(value, axis):
    return lax.ppermute(value, axis, [(0, 1), (1, 0)])


def passed_along(value, axis, steps):
    count = lax.axis_size(axis)
    pairs = [(source, (source + steps) % count) for source in range(count)]
    return lax.ppermute(value, axis, pairs)


def routing(ids, gates, experts, capacity):
    pairs = ids.reshape(-1)
    hot = (pairs[:, None] == jnp.arange(experts, dtype=jnp.int32)[None, :]).astype(jnp.int32)
    before = jnp.cumsum(hot, axis=0) - hot
    slot = jnp.sum(hot * before, axis=1)
    target = (pairs * capacity + slot).reshape(ids.shape)
    columns = jnp.arange(experts * capacity, dtype=jnp.int32)
    match = (target[:, :, None] == columns[None, None, :]).astype(jnp.float32)
    select = jnp.sum(match, axis=1).astype(jnp.bfloat16)
    weights = jnp.sum(gates[:, :, None] * match, axis=1)
    return (select, weights)


def into_slots(select, rows_in):
    placed = lax.dot_general(
        select, rows_in, (((0,), (0,)), ((), ())), preferred_element_type=jnp.float32
    )
    return placed.astype(jnp.bfloat16)


def forward_rows(rows_in, w_gate, w_up, w_down):
    g = jnp.dot(rows_in, w_gate, preferred_element_type=jnp.float32)
    u = jnp.dot(rows_in, w_up, preferred_element_type=jnp.float32)
    hidden = (g * jax.nn.sigmoid(g) * u).astype(jnp.bfloat16)
    return jnp.dot(hidden, w_down, preferred_element_type=jnp.float32).astype(jnp.bfloat16)


def backward_rows(rows_all, w_gate, w_up, w_down):
    width = w_gate.shape[0]
    rows_in = rows_all[:, :width]
    rows_grad = rows_all[:, width:]
    g = jnp.dot(rows_in, w_gate, preferred_element_type=jnp.float32)
    u = jnp.dot(rows_in, w_up, preferred_element_type=jnp.float32)
    dh = lax.dot_general(
        rows_grad, w_down, (((1,), (1,)), ((), ())), preferred_element_type=jnp.float32
    )
    sig = jax.nn.sigmoid(g)
    grad_gate = (dh * u * sig * (1.0 + g * (1.0 - sig))).astype(jnp.bfloat16)
    grad_up = (dh * g * sig).astype(jnp.bfloat16)
    part = lax.dot_general(
        grad_gate, w_gate, (((1,), (1,)), ((), ())), preferred_element_type=jnp.float32
    )
    part = part + lax.dot_general(
        grad_up, w_up, (((1,), (1,)), ((), ())), preferred_element_type=jnp.float32
    )
    return part.astype(jnp.bfloat16)


def dispatch(slots):
    count = lax.axis_size("z")
    pieces = []
    for d in range(count):
        if d == 0:
            received = slots[0]
        else:
            received = lax.ppermute(slots[d], "z", [(i, i ^ d) for i in range(count)])
        across = jnp.stack([received, swap(received, "x")])
        pieces.append(jnp.stack([across, swap(across, "c")]))
    return jnp.stack(pieces, axis=2)


def reduce_group(partial):
    from_core = swap(partial[1], "c")
    chip_sum = partial[0].astype(jnp.float32) + from_core.astype(jnp.float32)
    totals = []
    for d in range(chip_sum.shape[1]):
        from_x = swap(chip_sum[1, d].astype(jnp.bfloat16), "x")
        totals.append((chip_sum[0, d] + from_x.astype(jnp.float32)).astype(jnp.bfloat16))
    return totals


def returned(totals):
    count = lax.axis_size("z")
    out = [totals[0]]
    for d in range(1, count):
        out.append(lax.ppermute(totals[d], "z", [(i, i ^ d) for i in range(count)]))
    return jnp.stack(out)


def body(
    fwd_input,
    fwd_experts,
    fwd_gates,
    bwd_input,
    bwd_grad,
    bwd_experts,
    bwd_gates,
    gate_proj,
    up_proj,
    down_proj,
):
    experts = lax.axis_size("z")
    tokens = fwd_input.shape[1]
    width = fwd_input.shape[2]
    capacity = min(tokens, 3 * tokens * TOPK // (2 * experts))
    w_gate = gate_proj[0]
    w_up = up_proj[0]
    w_down = down_proj[0]
    here = lax.axis_index("z")
    f_select, f_weights = routing(fwd_experts[0] ^ here, fwd_gates[0], experts, capacity)
    b_select, b_weights = routing(bwd_experts[0] ^ here, bwd_gates[0], experts, capacity)
    f_slots = into_slots(f_select, fwd_input[0]).reshape(experts, capacity, width)
    b_joined = jnp.concatenate([bwd_input[0], bwd_grad[0]], axis=1)
    b_slots = into_slots(b_select, b_joined).reshape(experts, capacity, 2 * width)
    f_rows = dispatch(f_slots)
    b_rows = dispatch(b_slots)
    f_partial = forward_rows(f_rows.reshape(-1, width), w_gate, w_up, w_down)
    f_totals = reduce_group(f_partial.reshape(2, 2, experts, capacity, width))
    b_rows, f_totals = lax.optimization_barrier((b_rows, f_totals))
    f_out = returned(f_totals)
    b_partial = backward_rows(b_rows.reshape(-1, 2 * width), w_gate, w_up, w_down)
    b_totals = reduce_group(b_partial.reshape(2, 2, experts, capacity, width))
    b_totals, f_out = lax.optimization_barrier((b_totals, f_out))
    b_out = returned(b_totals)
    high = lax.Precision.HIGHEST
    f_mixed = jnp.dot(
        f_weights, f_out.reshape(experts * capacity, width).astype(jnp.float32), precision=high
    )
    f_result = (fwd_input[0].astype(jnp.float32) + f_mixed).astype(jnp.bfloat16)
    b_mixed = jnp.dot(
        b_weights, b_out.reshape(experts * capacity, width).astype(jnp.float32), precision=high
    )
    b_result = (bwd_grad[0].astype(jnp.float32) + b_mixed).astype(jnp.bfloat16)
    next_section_input = passed_along(f_result[None], "pp", 1)
    prev_section_grad = passed_along(b_result[None], "pp", -1)
    return (next_section_input, prev_section_grad)


def solution(mesh):
    sections = mesh.shape["pp"]
    devices = mesh.shape["ep"]
    grid = mesh.devices.reshape(sections, devices // GROUP, 2, 2)
    split = Mesh(grid, ("pp",) + EP)
    rows = P("pp", EP, None)
    columns = P("pp", None, EP)
    in_specs = (rows, rows, rows, rows, rows, rows, rows, columns, columns, rows)
    out_specs = (rows, rows)
    return jax.shard_map(body, mesh=split, in_specs=in_specs, out_specs=out_specs, check_vma=False)
```

```python
import jax
import jax.numpy as jnp
from jax import lax
from jax.sharding import Mesh
from jax.sharding import PartitionSpec as P

GROUP = 4
TOPK = 2
EP = ("z", "x", "c")


def swap(value, axis):
    return lax.ppermute(value, axis, [(0, 1), (1, 0)])


def passed_along(value, axis, steps):
    count = lax.axis_size(axis)
    pairs = [(source, (source + steps) % count) for source in range(count)]
    return lax.ppermute(value, axis, pairs)


def routing(ids, gates, experts, capacity):
    pairs = ids.reshape(-1)
    hot = (pairs[:, None] == jnp.arange(experts, dtype=jnp.int32)[None, :]).astype(jnp.int32)
    before = jnp.cumsum(hot, axis=0) - hot
    slot = jnp.sum(hot * before, axis=1)
    target = (pairs * capacity + slot).reshape(ids.shape)
    columns = jnp.arange(experts * capacity, dtype=jnp.int32)
    match = (target[:, :, None] == columns[None, None, :]).astype(jnp.float32)
    select = jnp.sum(match, axis=1).astype(jnp.bfloat16)
    weights = jnp.sum(gates[:, :, None] * match, axis=1)
    return (select, weights)


def into_slots(select, rows_in):
    placed = lax.dot_general(
        select, rows_in, (((0,), (0,)), ((), ())), preferred_element_type=jnp.float32
    )
    return placed.astype(jnp.bfloat16)


def forward_rows(rows_in, w_gate, w_up, w_down):
    g = jnp.dot(rows_in, w_gate, preferred_element_type=jnp.float32)
    u = jnp.dot(rows_in, w_up, preferred_element_type=jnp.float32)
    hidden = (g * jax.nn.sigmoid(g) * u).astype(jnp.bfloat16)
    return jnp.dot(hidden, w_down, preferred_element_type=jnp.float32).astype(jnp.bfloat16)


def backward_rows(rows_all, w_gate, w_up, w_down):
    width = w_gate.shape[0]
    rows_in = rows_all[:, :width]
    rows_grad = rows_all[:, width:]
    g = jnp.dot(rows_in, w_gate, preferred_element_type=jnp.float32)
    u = jnp.dot(rows_in, w_up, preferred_element_type=jnp.float32)
    dh = lax.dot_general(
        rows_grad, w_down, (((1,), (1,)), ((), ())), preferred_element_type=jnp.float32
    )
    sig = jax.nn.sigmoid(g)
    grad_gate = (dh * u * sig * (1.0 + g * (1.0 - sig))).astype(jnp.bfloat16)
    grad_up = (dh * g * sig).astype(jnp.bfloat16)
    part = lax.dot_general(
        grad_gate, w_gate, (((1,), (1,)), ((), ())), preferred_element_type=jnp.float32
    )
    part = part + lax.dot_general(
        grad_up, w_up, (((1,), (1,)), ((), ())), preferred_element_type=jnp.float32
    )
    return part.astype(jnp.bfloat16)


def dispatch(slots):
    count = lax.axis_size("z")
    pieces = []
    for d in range(count):
        if d == 0:
            received = slots[0]
        else:
            received = lax.ppermute(slots[d], "z", [(i, i ^ d) for i in range(count)])
        across = jnp.stack([received, swap(received, "x")])
        pieces.append(jnp.stack([across, swap(across, "c")]))
    return jnp.stack(pieces, axis=2)


def reduce_group(partial):
    from_core = swap(partial[1], "c")
    chip_sum = partial[0].astype(jnp.float32) + from_core.astype(jnp.float32)
    totals = []
    for d in range(chip_sum.shape[1]):
        from_x = swap(chip_sum[1, d].astype(jnp.bfloat16), "x")
        totals.append((chip_sum[0, d] + from_x.astype(jnp.float32)).astype(jnp.bfloat16))
    return totals


def returned(totals):
    count = lax.axis_size("z")
    out = [totals[0]]
    for d in range(1, count):
        out.append(lax.ppermute(totals[d], "z", [(i, i ^ d) for i in range(count)]))
    return jnp.stack(out)


def body(
    fwd_input,
    fwd_experts,
    fwd_gates,
    bwd_input,
    bwd_grad,
    bwd_experts,
    bwd_gates,
    gate_proj,
    up_proj,
    down_proj,
):
    experts = lax.axis_size("z")
    tokens = fwd_input.shape[1]
    width = fwd_input.shape[2]
    capacity = min(tokens, 3 * tokens * TOPK // (2 * experts))
    w_gate = gate_proj[0]
    w_up = up_proj[0]
    w_down = down_proj[0]
    here = lax.axis_index("z")
    f_select, f_weights = routing(fwd_experts[0] ^ here, fwd_gates[0], experts, capacity)
    b_select, b_weights = routing(bwd_experts[0] ^ here, bwd_gates[0], experts, capacity)
    f_slots = into_slots(f_select, fwd_input[0]).reshape(experts, capacity, width)
    b_joined = jnp.concatenate([bwd_input[0], bwd_grad[0]], axis=1)
    b_slots = into_slots(b_select, b_joined).reshape(experts, capacity, 2 * width)
    f_rows = dispatch(f_slots)
    b_rows = dispatch(b_slots)
    f_partial = forward_rows(f_rows.reshape(-1, width), w_gate, w_up, w_down)
    f_totals = reduce_group(f_partial.reshape(2, 2, experts, capacity, width))
    b_rows, f_totals = lax.optimization_barrier((b_rows, f_totals))
    f_out = returned(f_totals)
    b_partial = backward_rows(b_rows.reshape(-1, 2 * width), w_gate, w_up, w_down)
    b_totals = reduce_group(b_partial.reshape(2, 2, experts, capacity, width))
    high = lax.Precision.HIGHEST
    f_mixed = jnp.dot(
        f_weights, f_out.reshape(experts * capacity, width).astype(jnp.float32), precision=high
    )
    f_result = (fwd_input[0].astype(jnp.float32) + f_mixed).astype(jnp.bfloat16)
    next_section_input = passed_along(f_result[None], "pp", 1)
    b_totals, next_section_input = lax.optimization_barrier((b_totals, next_section_input))
    b_out = returned(b_totals)
    b_mixed = jnp.dot(
        b_weights, b_out.reshape(experts * capacity, width).astype(jnp.float32), precision=high
    )
    b_result = (bwd_grad[0].astype(jnp.float32) + b_mixed).astype(jnp.bfloat16)
    prev_section_grad = passed_along(b_result[None], "pp", -1)
    return (next_section_input, prev_section_grad)


def solution(mesh):
    sections = mesh.shape["pp"]
    devices = mesh.shape["ep"]
    grid = mesh.devices.reshape(sections, devices // GROUP, 2, 2)
    split = Mesh(grid, ("pp",) + EP)
    rows = P("pp", EP, None)
    columns = P("pp", None, EP)
    in_specs = (rows, rows, rows, rows, rows, rows, rows, columns, columns, rows)
    out_specs = (rows, rows)
    return jax.shard_map(body, mesh=split, in_specs=in_specs, out_specs=out_specs, check_vma=False)
```

```python
import jax
import jax.numpy as jnp
from jax import lax
from jax.sharding import Mesh
from jax.sharding import PartitionSpec as P

GROUP = 4
TOPK = 2
EP = ("z", "x", "c")


def swap(value, axis):
    return lax.ppermute(value, axis, [(0, 1), (1, 0)])


def passed_along(value, axis, steps):
    count = lax.axis_size(axis)
    pairs = [(source, (source + steps) % count) for source in range(count)]
    return lax.ppermute(value, axis, pairs)


def routing(ids, gates, experts, capacity):
    pairs = ids.reshape(-1)
    hot = (pairs[:, None] == jnp.arange(experts, dtype=jnp.int32)[None, :]).astype(jnp.int32)
    before = jnp.cumsum(hot, axis=0) - hot
    slot = jnp.sum(hot * before, axis=1)
    target = (pairs * capacity + slot).reshape(ids.shape)
    columns = jnp.arange(experts * capacity, dtype=jnp.int32)
    match = (target[:, :, None] == columns[None, None, :]).astype(jnp.float32)
    select = jnp.sum(match, axis=1).astype(jnp.bfloat16)
    weights = jnp.sum(gates[:, :, None] * match, axis=1)
    return (select, weights)


def into_slots(select, rows_in):
    placed = lax.dot_general(
        select, rows_in, (((0,), (0,)), ((), ())), preferred_element_type=jnp.float32
    )
    return placed.astype(jnp.bfloat16)


def forward_rows(rows_in, w_gate, w_up, w_down):
    g = jnp.dot(rows_in, w_gate, preferred_element_type=jnp.float32)
    u = jnp.dot(rows_in, w_up, preferred_element_type=jnp.float32)
    hidden = (g * jax.nn.sigmoid(g) * u).astype(jnp.bfloat16)
    return jnp.dot(hidden, w_down, preferred_element_type=jnp.float32).astype(jnp.bfloat16)


def backward_rows(rows_all, w_gate, w_up, w_down):
    width = w_gate.shape[0]
    rows_in = rows_all[:, :width]
    rows_grad = rows_all[:, width:]
    g = jnp.dot(rows_in, w_gate, preferred_element_type=jnp.float32)
    u = jnp.dot(rows_in, w_up, preferred_element_type=jnp.float32)
    dh = lax.dot_general(
        rows_grad, w_down, (((1,), (1,)), ((), ())), preferred_element_type=jnp.float32
    )
    sig = jax.nn.sigmoid(g)
    grad_gate = (dh * u * sig * (1.0 + g * (1.0 - sig))).astype(jnp.bfloat16)
    grad_up = (dh * g * sig).astype(jnp.bfloat16)
    part = lax.dot_general(
        grad_gate, w_gate, (((1,), (1,)), ((), ())), preferred_element_type=jnp.float32
    )
    part = part + lax.dot_general(
        grad_up, w_up, (((1,), (1,)), ((), ())), preferred_element_type=jnp.float32
    )
    return part.astype(jnp.bfloat16)


def z_round(chunk, d):
    count = lax.axis_size("z")
    if d == 0:
        return chunk
    return lax.ppermute(chunk, "z", [(i, i ^ d) for i in range(count)])


def spread(received):
    across = jnp.stack([received, swap(received, "x")])
    return jnp.stack([across, swap(across, "c")])


def reduce_group(partial):
    from_core = swap(partial[1], "c")
    chip_sum = partial[0].astype(jnp.float32) + from_core.astype(jnp.float32)
    totals = []
    for d in range(chip_sum.shape[1]):
        from_x = swap(chip_sum[1, d].astype(jnp.bfloat16), "x")
        totals.append((chip_sum[0, d] + from_x.astype(jnp.float32)).astype(jnp.bfloat16))
    return totals


def returned(totals):
    count = lax.axis_size("z")
    out = [totals[0]]
    for d in range(1, count):
        out.append(lax.ppermute(totals[d], "z", [(i, i ^ d) for i in range(count)]))
    return jnp.stack(out)


def body(
    fwd_input,
    fwd_experts,
    fwd_gates,
    bwd_input,
    bwd_grad,
    bwd_experts,
    bwd_gates,
    gate_proj,
    up_proj,
    down_proj,
):
    experts = lax.axis_size("z")
    tokens = fwd_input.shape[1]
    width = fwd_input.shape[2]
    capacity = min(tokens, 3 * tokens * TOPK // (2 * experts))
    w_gate = gate_proj[0]
    w_up = up_proj[0]
    w_down = down_proj[0]
    here = lax.axis_index("z")
    f_select, f_weights = routing(fwd_experts[0] ^ here, fwd_gates[0], experts, capacity)
    b_select, b_weights = routing(bwd_experts[0] ^ here, bwd_gates[0], experts, capacity)
    f_slots = into_slots(f_select, fwd_input[0]).reshape(experts, capacity, width)
    b_joined = jnp.concatenate([bwd_input[0], bwd_grad[0]], axis=1)
    b_slots = into_slots(b_select, b_joined).reshape(experts, capacity, 2 * width)
    early = experts // 2
    f_rows = jnp.stack([spread(z_round(f_slots[d], d)) for d in range(experts)], axis=2)
    b_received = [z_round(b_slots[d], d) for d in range(experts)]
    b_near = [spread(r) for r in b_received[:early]]
    f_partial = forward_rows(f_rows.reshape(-1, width), w_gate, w_up, w_down)
    f_totals = reduce_group(f_partial.reshape(2, 2, experts, capacity, width))
    b_far, f_totals = lax.optimization_barrier((tuple(b_received[early:]), f_totals))
    b_rows = jnp.stack(b_near + [spread(r) for r in b_far], axis=2)
    f_out = returned(f_totals)
    b_partial = backward_rows(b_rows.reshape(-1, 2 * width), w_gate, w_up, w_down)
    b_totals = reduce_group(b_partial.reshape(2, 2, experts, capacity, width))
    b_totals, f_out = lax.optimization_barrier((b_totals, f_out))
    b_out = returned(b_totals)
    high = lax.Precision.HIGHEST
    f_mixed = jnp.dot(
        f_weights, f_out.reshape(experts * capacity, width).astype(jnp.float32), precision=high
    )
    f_result = (fwd_input[0].astype(jnp.float32) + f_mixed).astype(jnp.bfloat16)
    b_mixed = jnp.dot(
        b_weights, b_out.reshape(experts * capacity, width).astype(jnp.float32), precision=high
    )
    b_result = (bwd_grad[0].astype(jnp.float32) + b_mixed).astype(jnp.bfloat16)
    next_section_input = passed_along(f_result[None], "pp", 1)
    prev_section_grad = passed_along(b_result[None], "pp", -1)
    return (next_section_input, prev_section_grad)


def solution(mesh):
    sections = mesh.shape["pp"]
    devices = mesh.shape["ep"]
    grid = mesh.devices.reshape(sections, devices // GROUP, 2, 2)
    split = Mesh(grid, ("pp",) + EP)
    rows = P("pp", EP, None)
    columns = P("pp", None, EP)
    in_specs = (rows, rows, rows, rows, rows, rows, rows, columns, columns, rows)
    out_specs = (rows, rows)
    return jax.shard_map(body, mesh=split, in_specs=in_specs, out_specs=out_specs, check_vma=False)
```

```python
import jax
import jax.numpy as jnp
from jax import lax
from jax.sharding import Mesh
from jax.sharding import PartitionSpec as P

GROUP = 4
TOPK = 2
EP = ("z", "x", "c")


def swap(value, axis):
    return lax.ppermute(value, axis, [(0, 1), (1, 0)])


def passed_along(value, axis, steps):
    count = lax.axis_size(axis)
    pairs = [(source, (source + steps) % count) for source in range(count)]
    return lax.ppermute(value, axis, pairs)


def routing(ids, gates, experts, capacity):
    pairs = ids.reshape(-1)
    hot = (pairs[:, None] == jnp.arange(experts, dtype=jnp.int32)[None, :]).astype(jnp.int32)
    before = jnp.cumsum(hot, axis=0) - hot
    slot = jnp.sum(hot * before, axis=1)
    target = (pairs * capacity + slot).reshape(ids.shape)
    columns = jnp.arange(experts * capacity, dtype=jnp.int32)
    match = (target[:, :, None] == columns[None, None, :]).astype(jnp.float32)
    select = jnp.sum(match, axis=1).astype(jnp.bfloat16)
    weights = jnp.sum(gates[:, :, None] * match, axis=1)
    return (select, weights)


def into_slots(select, rows_in):
    placed = lax.dot_general(
        select, rows_in, (((0,), (0,)), ((), ())), preferred_element_type=jnp.float32
    )
    return placed.astype(jnp.bfloat16)


def forward_rows(rows_in, w_gate, w_up, w_down):
    g = jnp.dot(rows_in, w_gate, preferred_element_type=jnp.float32)
    u = jnp.dot(rows_in, w_up, preferred_element_type=jnp.float32)
    hidden = (g * jax.nn.sigmoid(g) * u).astype(jnp.bfloat16)
    return jnp.dot(hidden, w_down, preferred_element_type=jnp.float32).astype(jnp.bfloat16)


def backward_rows(rows_all, w_gate, w_up, w_down):
    width = w_gate.shape[0]
    rows_in = rows_all[:, :width]
    rows_grad = rows_all[:, width:]
    g = jnp.dot(rows_in, w_gate, preferred_element_type=jnp.float32)
    u = jnp.dot(rows_in, w_up, preferred_element_type=jnp.float32)
    dh = lax.dot_general(
        rows_grad, w_down, (((1,), (1,)), ((), ())), preferred_element_type=jnp.float32
    )
    sig = jax.nn.sigmoid(g)
    grad_gate = (dh * u * sig * (1.0 + g * (1.0 - sig))).astype(jnp.bfloat16)
    grad_up = (dh * g * sig).astype(jnp.bfloat16)
    part = lax.dot_general(
        grad_gate, w_gate, (((1,), (1,)), ((), ())), preferred_element_type=jnp.float32
    )
    part = part + lax.dot_general(
        grad_up, w_up, (((1,), (1,)), ((), ())), preferred_element_type=jnp.float32
    )
    return part.astype(jnp.bfloat16)


def dispatch(slots):
    count = lax.axis_size("z")
    pieces = []
    for d in range(count):
        if d == 0:
            received = slots[0]
        else:
            received = lax.ppermute(slots[d], "z", [(i, i ^ d) for i in range(count)])
        across = jnp.stack([received, swap(received, "x")])
        pieces.append(jnp.stack([across, swap(across, "c")]))
    return jnp.stack(pieces, axis=2)


def reduce_group(partial):
    from_core = swap(partial[1], "c")
    chip_sum = partial[0].astype(jnp.float32) + from_core.astype(jnp.float32)
    totals = []
    for d in range(chip_sum.shape[1]):
        from_x = swap(chip_sum[1, d].astype(jnp.bfloat16), "x")
        totals.append((chip_sum[0, d] + from_x.astype(jnp.float32)).astype(jnp.bfloat16))
    return totals


def returned(totals):
    count = lax.axis_size("z")
    out = [totals[0]]
    for d in range(1, count):
        out.append(lax.ppermute(totals[d], "z", [(i, i ^ d) for i in range(count)]))
    return jnp.stack(out)


def body(
    fwd_input,
    fwd_experts,
    fwd_gates,
    bwd_input,
    bwd_grad,
    bwd_experts,
    bwd_gates,
    gate_proj,
    up_proj,
    down_proj,
):
    experts = lax.axis_size("z")
    tokens = fwd_input.shape[1]
    width = fwd_input.shape[2]
    capacity = min(tokens, 3 * tokens * TOPK // (2 * experts))
    w_gate = gate_proj[0]
    w_up = up_proj[0]
    w_down = down_proj[0]
    here = lax.axis_index("z")
    f_select, f_weights = routing(fwd_experts[0] ^ here, fwd_gates[0], experts, capacity)
    b_select, b_weights = routing(bwd_experts[0] ^ here, bwd_gates[0], experts, capacity)
    f_slots = into_slots(f_select, fwd_input[0]).reshape(experts, capacity, width)
    b_joined = jnp.concatenate([bwd_input[0], bwd_grad[0]], axis=1)
    b_slots = into_slots(b_select, b_joined).reshape(experts, capacity, 2 * width)
    f_rows = dispatch(f_slots)
    b_rows = dispatch(b_slots)
    f_partial = forward_rows(f_rows.reshape(-1, width), w_gate, w_up, w_down)
    f_totals = reduce_group(f_partial.reshape(2, 2, experts, capacity, width))
    b_rows, f_totals = lax.optimization_barrier((b_rows, f_totals))
    f_out = returned(f_totals)
    b_partial = backward_rows(b_rows.reshape(-1, 2 * width), w_gate, w_up, w_down)
    b_sum = reduce_group(b_partial.reshape(2, 2, experts, capacity, width)[:, :, None])
    b_totals = list(b_sum[0])
    b_totals, f_out = lax.optimization_barrier((b_totals, f_out))
    b_out = returned(b_totals)
    high = lax.Precision.HIGHEST
    f_mixed = jnp.dot(
        f_weights, f_out.reshape(experts * capacity, width).astype(jnp.float32), precision=high
    )
    f_result = (fwd_input[0].astype(jnp.float32) + f_mixed).astype(jnp.bfloat16)
    b_mixed = jnp.dot(
        b_weights, b_out.reshape(experts * capacity, width).astype(jnp.float32), precision=high
    )
    b_result = (bwd_grad[0].astype(jnp.float32) + b_mixed).astype(jnp.bfloat16)
    next_section_input = passed_along(f_result[None], "pp", 1)
    prev_section_grad = passed_along(b_result[None], "pp", -1)
    return (next_section_input, prev_section_grad)


def solution(mesh):
    sections = mesh.shape["pp"]
    devices = mesh.shape["ep"]
    grid = mesh.devices.reshape(sections, devices // GROUP, 2, 2)
    split = Mesh(grid, ("pp",) + EP)
    rows = P("pp", EP, None)
    columns = P("pp", None, EP)
    in_specs = (rows, rows, rows, rows, rows, rows, rows, columns, columns, rows)
    out_specs = (rows, rows)
    return jax.shard_map(body, mesh=split, in_specs=in_specs, out_specs=out_specs, check_vma=False)
```
